256 devices in a mesh: space: 32 (over y_lo, z, core), chan: 8 (over x, y_hi).
Axes of the slice: x: 4, y: 4 (y_hi: 2, y_lo: 2; y = y_hi * 2 + y_lo), z: 8, core: 2. Of those that a mesh axis runs over, the one named last changes fastest.
Arguments:
- inputs: bfloat16 [32, 256, 2048], P('space', 'chan'), may hold values from -6 to 6
- weights: bfloat16 [27, 256, 256], P(None, 'chan'), may hold values from -0.078125 to 0.078125
- cotangent: bfloat16 [32, 256, 2048], P('space', 'chan'), may hold values from -6 to 6
Outputs:
- output: bfloat16 [32, 256, 2048], P('space', 'chan')
- input_grad: bfloat16 [32, 256, 2048], P('space', 'chan')
- weight_grad: float32 [27, 256, 256], P(None, 'chan')
The draws below stay inside these ranges and needn't reach their ends.
All inputs are finite; a program needn't handle non-finite values.
Results may differ from the reference program's by a relative error of at most 0.001.
Values may be sent and summed in bfloat16 or wider, within the bound.
No kernel may reach another device: no remote copies, remote signals or barrier semaphores. Data moves between devices by JAX's collectives and lax.ppermute only.
A program may use at most 192 MiB of HBM per device.

```python
import jax
import jax.numpy as jnp
from jax import lax

CIN = 256
COUT = 256
PLANE_ROWS = 32
ROW_CELLS = 64
DEPTH = 32
CELLS = 2048


def block_scale(own_key, extent, shards, low, top_value):
    def one(axis_at, parts):
        steps = jax.random.uniform(jax.random.fold_in(jax.random.fold_in(own_key, 6), axis_at), (parts,), jnp.float32, low / len(shards), top_value / len(shards))
        return jnp.repeat(jnp.exp(steps), extent[axis_at] // parts).reshape((-1,) + (1,) * (len(extent) - axis_at - 1))

    gain = one(*shards[0])
    for cut in shards[1:]:
        gain = gain * one(*cut)
    return gain


def scatter_about(key, shape, scale, most, shards=(), kind=jnp.bfloat16):
    factor_of = block_scale(key, shape, shards, -0.22, 0.18) if shards else 1.0
    values = jax.random.normal(key, shape, jnp.float32) * scale * factor_of
    return jnp.minimum(jnp.maximum(values, -most), most).astype(kind)


def setup_inputs(seed: int = 0) -> dict:
    splits = jax.random.split(jax.random.key(seed), 4)
    return {
        "inputs": scatter_about(splits[0], (DEPTH, CIN, CELLS), 1.0, 6.0, ((0, 32), (1, 8))),
        "weights": scatter_about(splits[1], (27, CIN, COUT), (27 * CIN) ** -0.5, 0.078125, ((1, 8),)),
        "cotangent": scatter_about(splits[2], (DEPTH, COUT, CELLS), 1.0, 6.0, ((0, 32), (1, 8))),
    }


def conv_volume(inputs_f, weights_f):
    lhs = inputs_f.reshape(DEPTH, CIN, PLANE_ROWS, ROW_CELLS).transpose(1, 0, 2, 3)[None]
    rhs = weights_f.reshape(3, 3, 3, CIN, COUT).transpose(4, 3, 0, 1, 2)
    result = lax.conv_general_dilated(lhs, rhs, (1, 1, 1), [(1, 1), (1, 1), (1, 1)], dimension_numbers=('NCDHW', 'OIDHW', 'NCDHW'), precision=lax.Precision.HIGHEST)
    return result[0].transpose(1, 0, 2, 3).reshape(DEPTH, COUT, PLANE_ROWS * ROW_CELLS)

def reference(inputs, weights, cotangent):
    inputs_f = inputs.astype(jnp.float32)
    weights_f = weights.astype(jnp.float32)
    result, pullback = jax.vjp(conv_volume, inputs_f, weights_f)
    input_grad, weight_grad = pullback(cotangent.astype(jnp.float32))
    return (result.astype(jnp.bfloat16), input_grad.astype(jnp.bfloat16), weight_grad.astype(jnp.float32))
```

```python
import jax
import jax.numpy as jnp
from jax import lax
from jax.sharding import PartitionSpec as P

PLANE_ROWS = 32
ROW_CELLS = 64


def extended(block, sides, width):
    for axis, dim in sides:
        count = lax.axis_size(axis)
        forward = [(i, i + 1) for i in range(count - 1)]
        backward = [(target, source) for source, target in forward]
        low = lax.ppermute(
            lax.slice_in_dim(block, block.shape[dim] - width, None, axis=dim), axis, forward
        )
        high = lax.ppermute(lax.slice_in_dim(block, 0, width, axis=dim), axis, backward)
        block = jnp.concatenate([low, block, high], axis=dim)
    return block


def partner_masks(count, first):
    masks = [1 << b for b in range(count.bit_length() - 1)]
    return [first] + [m for m in masks if m != first]


def halving_sum(block, axis, masks, dim):
    count = lax.axis_size(axis)
    index = lax.axis_index(axis)
    for mask in masks:
        half = block.shape[dim] // 2
        upper = (index // mask) % 2 == 1
        low = lax.slice_in_dim(block, 0, half, axis=dim)
        high = lax.slice_in_dim(block, half, 2 * half, axis=dim)
        keep = jnp.where(upper, high, low)
        send = jnp.where(upper, low, high)
        block = keep + lax.ppermute(send, axis, [(i, i ^ mask) for i in range(count)])
    return block


def doubling_gather(block, axis, masks, dim):
    count = lax.axis_size(axis)
    index = lax.axis_index(axis)
    for mask in masks:
        upper = (index // mask) % 2 == 1
        other = lax.ppermute(block, axis, [(i, i ^ mask) for i in range(count)])
        block = jnp.concatenate(
            [jnp.where(upper, other, block), jnp.where(upper, block, other)], axis=dim
        )
    return block


def plane_shift(field, tap_row, tap_col):
    lead = field.shape[:-1]
    grid = field.reshape(lead + (PLANE_ROWS, ROW_CELLS))
    padded = jnp.pad(grid, [(0, 0)] * len(lead) + [(1, 1), (1, 1)])
    window = padded[..., tap_row : tap_row + PLANE_ROWS, tap_col : tap_col + ROW_CELLS]
    return window.reshape(lead + (PLANE_ROWS * ROW_CELLS,))


def stack_at(padded, tap_row, tap_col):
    planes = padded.shape[0] - 2
    moved = plane_shift(padded, tap_row, tap_col)
    return jnp.concatenate(
        [moved[tap_depth : tap_depth + planes] for tap_depth in range(3)], axis=1
    )


def tap_weights(taps, tap_row, tap_col):
    return jnp.concatenate(
        [taps[tap_depth * 9 + tap_row * 3 + tap_col] for tap_depth in range(3)], axis=0
    )


def convolve(padded, taps):
    total = None
    for tap_row in range(3):
        for tap_col in range(3):
            term = jnp.einsum(
                "dcp,co->dop",
                stack_at(padded, tap_row, tap_col),
                tap_weights(taps, tap_row, tap_col),
                preferred_element_type=jnp.float32,
            )
            total = term if total is None else total + term
    return total


def weight_terms(padded, cot_whole, channels):
    pieces = [None] * 27
    for tap_row in range(3):
        for tap_col in range(3):
            block = jnp.einsum(
                "dcp,dop->co",
                stack_at(padded, tap_row, tap_col),
                cot_whole,
                preferred_element_type=jnp.float32,
            )
            block = block.reshape(3, channels, cot_whole.shape[1])
            for tap_depth in range(3):
                pieces[tap_depth * 9 + tap_row * 3 + tap_col] = block[tap_depth]
    return jnp.stack(pieces, axis=0)


def local(inputs, weights, cotangent):
    padded = extended(inputs, (("space", 0),), 1)
    partial_out = convolve(padded, weights)
    chan_masks = partner_masks(lax.axis_size("chan"), 1)[::-1]
    output = halving_sum(partial_out, "chan", chan_masks, 1).astype(jnp.bfloat16)
    gathered = lax.all_gather(cotangent, "chan", axis=1, tiled=True)
    cot_padded = extended(gathered, (("space", 0),), 1)
    cot_whole = cot_padded[1:-1]
    flipped = jnp.transpose(weights[::-1], (0, 2, 1))
    input_grad = convolve(cot_padded, flipped).astype(jnp.bfloat16)
    local_terms = weight_terms(padded, cot_whole, inputs.shape[1])
    space_masks = partner_masks(lax.axis_size("space"), 1)
    space_masks = [space_masks[0], space_masks[-1]] + space_masks[1:-1]
    flat = local_terms.reshape(-1, local_terms.shape[-1])
    flat = doubling_gather(halving_sum(flat, "space", space_masks, 0), "space", space_masks[::-1], 0)
    weight_grad = flat.reshape(local_terms.shape)
    return (output, input_grad, weight_grad)


def solution(mesh):
    placed = (P("space", "chan", None), P(None, "chan", None), P("space", "chan", None))
    return jax.shard_map(
        local,
        mesh=mesh,
        in_specs=placed,
        out_specs=(P("space", "chan", None), P("space", "chan", None), P(None, "chan", None)),
        check_vma=False,
    )
```

```python
import jax
import jax.numpy as jnp
from jax import lax
from jax.sharding import PartitionSpec as P

PLANE_ROWS = 32
ROW_CELLS = 64


def extended(block, sides, width):
    for axis, dim in sides:
        count = lax.axis_size(axis)
        forward = [(i, i + 1) for i in range(count - 1)]
        backward = [(target, source) for source, target in forward]
        low = lax.ppermute(
            lax.slice_in_dim(block, block.shape[dim] - width, None, axis=dim), axis, forward
        )
        high = lax.ppermute(lax.slice_in_dim(block, 0, width, axis=dim), axis, backward)
        block = jnp.concatenate([low, block, high], axis=dim)
    return block


def partner_masks(count, first):
    masks = [1 << b for b in range(count.bit_length() - 1)]
    return [first] + [m for m in masks if m != first]


def halving_sum(block, axis, masks, dim):
    count = lax.axis_size(axis)
    index = lax.axis_index(axis)
    for mask in masks:
        half = block.shape[dim] // 2
        upper = (index // mask) % 2 == 1
        low = lax.slice_in_dim(block, 0, half, axis=dim)
        high = lax.slice_in_dim(block, half, 2 * half, axis=dim)
        keep = jnp.where(upper, high, low)
        send = jnp.where(upper, low, high)
        block = keep + lax.ppermute(send, axis, [(i, i ^ mask) for i in range(count)])
    return block


def doubling_gather(block, axis, masks, dim):
    count = lax.axis_size(axis)
    index = lax.axis_index(axis)
    for mask in masks:
        upper = (index // mask) % 2 == 1
        other = lax.ppermute(block, axis, [(i, i ^ mask) for i in range(count)])
        block = jnp.concatenate(
            [jnp.where(upper, other, block), jnp.where(upper, block, other)], axis=dim
        )
    return block


def plane_shift(field, tap_row, tap_col):
    lead = field.shape[:-1]
    grid = field.reshape(lead + (PLANE_ROWS, ROW_CELLS))
    padded = jnp.pad(grid, [(0, 0)] * len(lead) + [(1, 1), (1, 1)])
    window = padded[..., tap_row : tap_row + PLANE_ROWS, tap_col : tap_col + ROW_CELLS]
    return window.reshape(lead + (PLANE_ROWS * ROW_CELLS,))


def stack_at(padded, tap_row, tap_col):
    planes = padded.shape[0] - 2
    moved = plane_shift(padded, tap_row, tap_col)
    return jnp.concatenate(
        [moved[tap_depth : tap_depth + planes] for tap_depth in range(3)], axis=1
    )


def tap_weights(taps, tap_row, tap_col):
    return jnp.concatenate(
        [taps[tap_depth * 9 + tap_row * 3 + tap_col] for tap_depth in range(3)], axis=0
    )


def convolve(padded, taps):
    total = None
    for tap_row in range(3):
        for tap_col in range(3):
            term = jnp.einsum(
                "dcp,co->dop",
                stack_at(padded, tap_row, tap_col),
                tap_weights(taps, tap_row, tap_col),
                preferred_element_type=jnp.float32,
            )
            total = term if total is None else total + term
    return total


def weight_terms(padded, cot_whole, channels):
    pieces = [None] * 27
    for tap_row in range(3):
        for tap_col in range(3):
            block = jnp.einsum(
                "dcp,dop->co",
                stack_at(padded, tap_row, tap_col),
                cot_whole,
                preferred_element_type=jnp.float32,
            )
            block = block.reshape(3, channels, cot_whole.shape[1])
            for tap_depth in range(3):
                pieces[tap_depth * 9 + tap_row * 3 + tap_col] = block[tap_depth]
    return jnp.stack(pieces, axis=0)


def conv_forward(padded, taps):
    planes, channels, cells = padded.shape
    lhs = padded.reshape(1, planes, channels, PLANE_ROWS, ROW_CELLS)
    rhs = taps.reshape(3, 3, 3, channels, taps.shape[-1])
    out = lax.conv_general_dilated(
        lhs, rhs, (1, 1, 1), [(0, 0), (1, 1), (1, 1)],
        dimension_numbers=("NDCHW", "DHWIO", "NDCHW"),
        preferred_element_type=jnp.float32,
    )
    return out.reshape(planes - 2, taps.shape[-1], cells)


def conv_backward(cot_padded, taps):
    planes, channels, cells = cot_padded.shape
    lhs = cot_padded.reshape(1, planes, channels, PLANE_ROWS, ROW_CELLS)
    rhs = taps.reshape(3, 3, 3, taps.shape[1], channels)[::-1, ::-1, ::-1]
    out = lax.conv_general_dilated(
        lhs, rhs, (1, 1, 1), [(0, 0), (1, 1), (1, 1)],
        dimension_numbers=("NDCHW", "DHWOI", "NDCHW"),
        preferred_element_type=jnp.float32,
    )
    return out.reshape(planes - 2, taps.shape[1], cells)


def conv_filter(padded, cot_whole):
    planes, channels, cells = padded.shape
    lhs = padded.reshape(planes, channels, 1, PLANE_ROWS, ROW_CELLS)
    rhs = cot_whole.reshape(planes - 2, cot_whole.shape[1], 1, PLANE_ROWS, ROW_CELLS)
    out = lax.conv_general_dilated(
        lhs, rhs, (1, 1, 1), [(0, 0), (1, 1), (1, 1)],
        dimension_numbers=("DNCHW", "DOIHW", "DHWNC"),
        preferred_element_type=jnp.float32,
    )
    return out.reshape(27, channels, cot_whole.shape[1])


def local(inputs, weights, cotangent):
    padded = extended(inputs, (("space", 0),), 1)
    partial_out = conv_forward(padded, weights)
    chan_masks = partner_masks(lax.axis_size("chan"), 1)
    output = halving_sum(partial_out, "chan", chan_masks[::-1], 1).astype(jnp.bfloat16)
    gathered = doubling_gather(cotangent, "chan", chan_masks, 1)
    cot_padded = extended(gathered, (("space", 0),), 1)
    cot_whole = cot_padded[1:-1]
    input_grad = conv_backward(cot_padded, weights).astype(jnp.bfloat16)
    local_terms = conv_filter(padded, cot_whole)
    space_masks = partner_masks(lax.axis_size("space"), 1)
    space_masks = [space_masks[0], space_masks[-1]] + space_masks[1:-1]
    flat = local_terms.reshape(-1, local_terms.shape[-1])
    flat = doubling_gather(halving_sum(flat, "space", space_masks, 0), "space", space_masks[::-1], 0)
    weight_grad = flat.reshape(local_terms.shape)
    return (output, input_grad, weight_grad)


def solution(mesh):
    placed = (P("space", "chan", None), P(None, "chan", None), P("space", "chan", None))
    return jax.shard_map(
        local,
        mesh=mesh,
        in_specs=placed,
        out_specs=(P("space", "chan", None), P("space", "chan", None), P(None, "chan", None)),
        check_vma=False,
    )
```

```python
import jax
import jax.numpy as jnp
from jax import lax
from jax.sharding import PartitionSpec as P

PLANE_ROWS = 32
ROW_CELLS = 64


def extended(block, sides, width):
    for axis, dim in sides:
        count = lax.axis_size(axis)
        forward = [(i, i + 1) for i in range(count - 1)]
        backward = [(target, source) for source, target in forward]
        low = lax.ppermute(
            lax.slice_in_dim(block, block.shape[dim] - width, None, axis=dim), axis, forward
        )
        high = lax.ppermute(lax.slice_in_dim(block, 0, width, axis=dim), axis, backward)
        block = jnp.concatenate([low, block, high], axis=dim)
    return block


def partner_masks(count, first):
    masks = [1 << b for b in range(count.bit_length() - 1)]
    return [first] + [m for m in masks if m != first]


def halving_sum(block, axis, masks, dim):
    count = lax.axis_size(axis)
    index = lax.axis_index(axis)
    for mask in masks:
        half = block.shape[dim] // 2
        upper = (index // mask) % 2 == 1
        low = lax.slice_in_dim(block, 0, half, axis=dim)
        high = lax.slice_in_dim(block, half, 2 * half, axis=dim)
        keep = jnp.where(upper, high, low)
        send = jnp.where(upper, low, high)
        block = keep + lax.ppermute(send, axis, [(i, i ^ mask) for i in range(count)])
    return block


def doubling_gather(block, axis, masks, dim):
    count = lax.axis_size(axis)
    index = lax.axis_index(axis)
    for mask in masks:
        upper = (index // mask) % 2 == 1
        other = lax.ppermute(block, axis, [(i, i ^ mask) for i in range(count)])
        block = jnp.concatenate(
            [jnp.where(upper, other, block), jnp.where(upper, block, other)], axis=dim
        )
    return block


def plane_shift(field, tap_row, tap_col):
    lead = field.shape[:-1]
    grid = field.reshape(lead + (PLANE_ROWS, ROW_CELLS))
    padded = jnp.pad(grid, [(0, 0)] * len(lead) + [(1, 1), (1, 1)])
    window = padded[..., tap_row : tap_row + PLANE_ROWS, tap_col : tap_col + ROW_CELLS]
    return window.reshape(lead + (PLANE_ROWS * ROW_CELLS,))


def stack_at(padded, tap_row, tap_col):
    planes = padded.shape[0] - 2
    moved = plane_shift(padded, tap_row, tap_col)
    return jnp.concatenate(
        [moved[tap_depth : tap_depth + planes] for tap_depth in range(3)], axis=1
    )


def tap_weights(taps, tap_row, tap_col):
    return jnp.concatenate(
        [taps[tap_depth * 9 + tap_row * 3 + tap_col] for tap_depth in range(3)], axis=0
    )


def convolve(padded, taps):
    total = None
    for tap_row in range(3):
        for tap_col in range(3):
            term = jnp.einsum(
                "dcp,co->dop",
                stack_at(padded, tap_row, tap_col),
                tap_weights(taps, tap_row, tap_col),
                preferred_element_type=jnp.float32,
            )
            total = term if total is None else total + term
    return total


def weight_terms(padded, cot_whole, channels):
    pieces = [None] * 27
    for tap_row in range(3):
        for tap_col in range(3):
            block = jnp.einsum(
                "dcp,dop->co",
                stack_at(padded, tap_row, tap_col),
                cot_whole,
                preferred_element_type=jnp.float32,
            )
            block = block.reshape(3, channels, cot_whole.shape[1])
            for tap_depth in range(3):
                pieces[tap_depth * 9 + tap_row * 3 + tap_col] = block[tap_depth]
    return jnp.stack(pieces, axis=0)


def conv_forward(padded, taps):
    planes, channels, cells = padded.shape
    lhs = padded.reshape(1, planes, channels, PLANE_ROWS, ROW_CELLS)
    rhs = taps.reshape(3, 3, 3, channels, taps.shape[-1])
    out = lax.conv_general_dilated(
        lhs, rhs, (1, 1, 1), [(0, 0), (1, 1), (1, 1)],
        dimension_numbers=("NDCHW", "DHWIO", "NDCHW"),
        preferred_element_type=jnp.float32,
    )
    return out.reshape(planes - 2, taps.shape[-1], cells)


def conv_backward(cot_padded, taps):
    planes, channels, cells = cot_padded.shape
    lhs = cot_padded.reshape(1, planes, channels, PLANE_ROWS, ROW_CELLS)
    rhs = taps.reshape(3, 3, 3, taps.shape[1], channels)[::-1, ::-1, ::-1]
    out = lax.conv_general_dilated(
        lhs, rhs, (1, 1, 1), [(0, 0), (1, 1), (1, 1)],
        dimension_numbers=("NDCHW", "DHWOI", "NDCHW"),
        preferred_element_type=jnp.float32,
    )
    return out.reshape(planes - 2, taps.shape[1], cells)


def conv_filter(padded, cot_whole):
    planes, channels, cells = padded.shape
    edge = ROW_CELLS + 1
    flat = jnp.pad(padded, ((0, 0), (0, 0), (edge, edge)))
    column = jnp.arange(cells) % ROW_CELLS
    pieces = []
    for tap_depth in range(3):
        for tap_row in range(3):
            for tap_col in range(3):
                offset = edge + (tap_row - 1) * ROW_CELLS + (tap_col - 1)
                moved = flat[tap_depth, :, offset : offset + cells]
                if tap_col == 0:
                    moved = jnp.where(column >= 1, moved, jnp.zeros_like(moved))
                if tap_col == 2:
                    moved = jnp.where(column < ROW_CELLS - 1, moved, jnp.zeros_like(moved))
                pieces.append(moved)
    stacked = jnp.stack(pieces, axis=0)
    return jnp.einsum(
        "kcp,op->kco", stacked, cot_whole[0], preferred_element_type=jnp.float32
    )


def scatter_sum(block, axis, dim):
    count = lax.axis_size(axis)
    shape = block.shape
    parts = block.reshape(shape[:dim] + (count, shape[dim] // count) + shape[dim + 1 :])
    parts = jnp.moveaxis(parts, dim, 0)
    parts = lax.all_to_all(parts, axis, 0, 0, tiled=True)
    return parts.sum(axis=0)


def spread_gather(block, axis, dim):
    count = lax.axis_size(axis)
    copies = jnp.broadcast_to(block[None], (count,) + block.shape)
    copies = lax.all_to_all(copies, axis, 0, 0, tiled=True)
    copies = jnp.moveaxis(copies, 0, dim)
    shape = block.shape
    return copies.reshape(shape[:dim] + (count * shape[dim],) + shape[dim + 1 :])


def local(inputs, weights, cotangent):
    padded = extended(inputs, (("space", 0),), 1)
    partial_out = conv_forward(padded, weights)
    output = scatter_sum(partial_out, "chan", 1).astype(jnp.bfloat16)
    gathered = spread_gather(cotangent, "chan", 1)
    cot_padded = extended(gathered, (("space", 0),), 1)
    cot_whole = cot_padded[1:-1]
    input_grad = conv_backward(cot_padded, weights).astype(jnp.bfloat16)
    local_terms = conv_filter(padded, cot_whole)
    flat = local_terms.reshape(-1, local_terms.shape[-1])
    flat = spread_gather(scatter_sum(flat, "space", 0), "space", 0)
    weight_grad = flat.reshape(local_terms.shape)
    return (output, input_grad, weight_grad)


def solution(mesh):
    placed = (P("space", "chan", None), P(None, "chan", None), P("space", "chan", None))
    return jax.shard_map(
        local,
        mesh=mesh,
        in_specs=placed,
        out_specs=(P("space", "chan", None), P("space", "chan", None), P(None, "chan", None)),
        check_vma=False,
    )
```

```python
import jax
import jax.numpy as jnp
from jax import lax
from jax.sharding import PartitionSpec as P

PLANE_ROWS = 32
ROW_CELLS = 64


def extended(block, sides, width):
    for axis, dim in sides:
        count = lax.axis_size(axis)
        forward = [(i, i + 1) for i in range(count - 1)]
        backward = [(target, source) for source, target in forward]
        low = lax.ppermute(
            lax.slice_in_dim(block, block.shape[dim] - width, None, axis=dim), axis, forward
        )
        high = lax.ppermute(lax.slice_in_dim(block, 0, width, axis=dim), axis, backward)
        block = jnp.concatenate([low, block, high], axis=dim)
    return block


def partner_masks(count, first):
    masks = [1 << b for b in range(count.bit_length() - 1)]
    return [first] + [m for m in masks if m != first]


def halving_sum(block, axis, masks, dim):
    count = lax.axis_size(axis)
    index = lax.axis_index(axis)
    for mask in masks:
        half = block.shape[dim] // 2
        upper = (index // mask) % 2 == 1
        low = lax.slice_in_dim(block, 0, half, axis=dim)
        high = lax.slice_in_dim(block, half, 2 * half, axis=dim)
        keep = jnp.where(upper, high, low)
        send = jnp.where(upper, low, high)
        block = keep + lax.ppermute(send, axis, [(i, i ^ mask) for i in range(count)])
    return block


def doubling_gather(block, axis, masks, dim):
    count = lax.axis_size(axis)
    index = lax.axis_index(axis)
    for mask in masks:
        upper = (index // mask) % 2 == 1
        other = lax.ppermute(block, axis, [(i, i ^ mask) for i in range(count)])
        block = jnp.concatenate(
            [jnp.where(upper, other, block), jnp.where(upper, block, other)], axis=dim
        )
    return block


def plane_shift(field, tap_row, tap_col):
    lead = field.shape[:-1]
    grid = field.reshape(lead + (PLANE_ROWS, ROW_CELLS))
    padded = jnp.pad(grid, [(0, 0)] * len(lead) + [(1, 1), (1, 1)])
    window = padded[..., tap_row : tap_row + PLANE_ROWS, tap_col : tap_col + ROW_CELLS]
    return window.reshape(lead + (PLANE_ROWS * ROW_CELLS,))


def stack_at(padded, tap_row, tap_col):
    planes = padded.shape[0] - 2
    moved = plane_shift(padded, tap_row, tap_col)
    return jnp.concatenate(
        [moved[tap_depth : tap_depth + planes] for tap_depth in range(3)], axis=1
    )


def tap_weights(taps, tap_row, tap_col):
    return jnp.concatenate(
        [taps[tap_depth * 9 + tap_row * 3 + tap_col] for tap_depth in range(3)], axis=0
    )


def convolve(padded, taps):
    total = None
    for tap_row in range(3):
        for tap_col in range(3):
            term = jnp.einsum(
                "dcp,co->dop",
                stack_at(padded, tap_row, tap_col),
                tap_weights(taps, tap_row, tap_col),
                preferred_element_type=jnp.float32,
            )
            total = term if total is None else total + term
    return total


def weight_terms(padded, cot_whole, channels):
    pieces = [None] * 27
    for tap_row in range(3):
        for tap_col in range(3):
            block = jnp.einsum(
                "dcp,dop->co",
                stack_at(padded, tap_row, tap_col),
                cot_whole,
                preferred_element_type=jnp.float32,
            )
            block = block.reshape(3, channels, cot_whole.shape[1])
            for tap_depth in range(3):
                pieces[tap_depth * 9 + tap_row * 3 + tap_col] = block[tap_depth]
    return jnp.stack(pieces, axis=0)


def conv_forward(padded, taps):
    planes, channels, cells = padded.shape
    lhs = padded.reshape(1, planes, channels, PLANE_ROWS, ROW_CELLS)
    rhs = taps.reshape(3, 3, 3, channels, taps.shape[-1])
    out = lax.conv_general_dilated(
        lhs, rhs, (1, 1, 1), [(0, 0), (1, 1), (1, 1)],
        dimension_numbers=("NDCHW", "DHWIO", "NDCHW"),
        preferred_element_type=jnp.float32,
    )
    return out.reshape(planes - 2, taps.shape[-1], cells)


def conv_backward(cot_padded, taps):
    planes, channels, cells = cot_padded.shape
    lhs = cot_padded.reshape(1, planes, channels, PLANE_ROWS, ROW_CELLS)
    rhs = taps.reshape(3, 3, 3, taps.shape[1], channels)[::-1, ::-1, ::-1]
    out = lax.conv_general_dilated(
        lhs, rhs, (1, 1, 1), [(0, 0), (1, 1), (1, 1)],
        dimension_numbers=("NDCHW", "DHWOI", "NDCHW"),
        preferred_element_type=jnp.float32,
    )
    return out.reshape(planes - 2, taps.shape[1], cells)


def conv_filter(padded, cot_whole):
    planes, channels, cells = padded.shape
    edge = ROW_CELLS + 1
    flat = jnp.pad(padded, ((0, 0), (0, 0), (edge, edge)))
    column = jnp.arange(cells) % ROW_CELLS
    pieces = []
    for tap_depth in range(3):
        for tap_row in range(3):
            for tap_col in range(3):
                offset = edge + (tap_row - 1) * ROW_CELLS + (tap_col - 1)
                moved = flat[tap_depth, :, offset : offset + cells]
                if tap_col == 0:
                    moved = jnp.where(column >= 1, moved, jnp.zeros_like(moved))
                if tap_col == 2:
                    moved = jnp.where(column < ROW_CELLS - 1, moved, jnp.zeros_like(moved))
                pieces.append(moved)
    stacked = jnp.stack(pieces, axis=0)
    return jnp.einsum(
        "kcp,op->kco", stacked, cot_whole[0], preferred_element_type=jnp.float32
    )


def scatter_sum(block, axis, dim):
    count = lax.axis_size(axis)
    shape = block.shape
    parts = block.reshape(shape[:dim] + (count, shape[dim] // count) + shape[dim + 1 :])
    parts = jnp.moveaxis(parts, dim, 0)
    parts = lax.all_to_all(parts, axis, 0, 0, tiled=True)
    return parts.sum(axis=0)


def spread_gather(block, axis, dim):
    count = lax.axis_size(axis)
    copies = jnp.broadcast_to(block[None], (count,) + block.shape)
    copies = lax.all_to_all(copies, axis, 0, 0, tiled=True)
    copies = jnp.moveaxis(copies, 0, dim)
    shape = block.shape
    return copies.reshape(shape[:dim] + (count * shape[dim],) + shape[dim + 1 :])


def swap_taps(taps, axis):
    count = lax.axis_size(axis)
    kinds, rows, cols = taps.shape
    parts = jnp.moveaxis(taps.reshape(kinds, rows, count, cols // count), 2, 0)
    parts = lax.all_to_all(parts, axis, 0, 0, tiled=True)
    return jnp.moveaxis(parts, 0, 1).reshape(kinds, count * rows, cols // count)


def local(inputs, weights, cotangent):
    gathered_in = spread_gather(inputs, "chan", 1)
    gathered = spread_gather(cotangent, "chan", 1)
    own_taps = swap_taps(weights, "chan")
    padded = extended(inputs, (("space", 0),), 1)
    in_padded = extended(gathered_in, (("space", 0),), 1)
    output = conv_forward(in_padded, own_taps).astype(jnp.bfloat16)
    cot_padded = extended(gathered, (("space", 0),), 1)
    input_grad = conv_backward(cot_padded, weights).astype(jnp.bfloat16)
    local_terms = conv_filter(padded, gathered)
    flat = local_terms.reshape(-1, local_terms.shape[-1])
    flat = spread_gather(scatter_sum(flat, "space", 0), "space", 0)
    weight_grad = flat.reshape(local_terms.shape)
    return (output, input_grad, weight_grad)


def solution(mesh):
    placed = (P("space", "chan", None), P(None, "chan", None), P("space", "chan", None))
    return jax.shard_map(
        local,
        mesh=mesh,
        in_specs=placed,
        out_specs=(P("space", "chan", None), P("space", "chan", None), P(None, "chan", None)),
        check_vma=False,
    )
```

```python
import jax
import jax.numpy as jnp
from jax import lax
from jax.sharding import PartitionSpec as P
from jax.experimental import pallas as pl
from jax.experimental.pallas import tpu as pltpu

PLANE_ROWS = 32
ROW_CELLS = 64


def extended(block, sides, width):
    for axis, dim in sides:
        count = lax.axis_size(axis)
        forward = [(i, i + 1) for i in range(count - 1)]
        backward = [(target, source) for source, target in forward]
        low = lax.ppermute(
            lax.slice_in_dim(block, block.shape[dim] - width, None, axis=dim), axis, forward
        )
        high = lax.ppermute(lax.slice_in_dim(block, 0, width, axis=dim), axis, backward)
        block = jnp.concatenate([low, block, high], axis=dim)
    return block


def partner_masks(count, first):
    masks = [1 << b for b in range(count.bit_length() - 1)]
    return [first] + [m for m in masks if m != first]


def halving_sum(block, axis, masks, dim):
    count = lax.axis_size(axis)
    index = lax.axis_index(axis)
    for mask in masks:
        half = block.shape[dim] // 2
        upper = (index // mask) % 2 == 1
        low = lax.slice_in_dim(block, 0, half, axis=dim)
        high = lax.slice_in_dim(block, half, 2 * half, axis=dim)
        keep = jnp.where(upper, high, low)
        send = jnp.where(upper, low, high)
        block = keep + lax.ppermute(send, axis, [(i, i ^ mask) for i in range(count)])
    return block


def doubling_gather(block, axis, masks, dim):
    count = lax.axis_size(axis)
    index = lax.axis_index(axis)
    for mask in masks:
        upper = (index // mask) % 2 == 1
        other = lax.ppermute(block, axis, [(i, i ^ mask) for i in range(count)])
        block = jnp.concatenate(
            [jnp.where(upper, other, block), jnp.where(upper, block, other)], axis=dim
        )
    return block


def plane_shift(field, tap_row, tap_col):
    lead = field.shape[:-1]
    grid = field.reshape(lead + (PLANE_ROWS, ROW_CELLS))
    padded = jnp.pad(grid, [(0, 0)] * len(lead) + [(1, 1), (1, 1)])
    window = padded[..., tap_row : tap_row + PLANE_ROWS, tap_col : tap_col + ROW_CELLS]
    return window.reshape(lead + (PLANE_ROWS * ROW_CELLS,))


def stack_at(padded, tap_row, tap_col):
    planes = padded.shape[0] - 2
    moved = plane_shift(padded, tap_row, tap_col)
    return jnp.concatenate(
        [moved[tap_depth : tap_depth + planes] for tap_depth in range(3)], axis=1
    )


def tap_weights(taps, tap_row, tap_col):
    return jnp.concatenate(
        [taps[tap_depth * 9 + tap_row * 3 + tap_col] for tap_depth in range(3)], axis=0
    )


def convolve(padded, taps):
    total = None
    for tap_row in range(3):
        for tap_col in range(3):
            term = jnp.einsum(
                "dcp,co->dop",
                stack_at(padded, tap_row, tap_col),
                tap_weights(taps, tap_row, tap_col),
                preferred_element_type=jnp.float32,
            )
            total = term if total is None else total + term
    return total


def weight_terms(padded, cot_whole, channels):
    pieces = [None] * 27
    for tap_row in range(3):
        for tap_col in range(3):
            block = jnp.einsum(
                "dcp,dop->co",
                stack_at(padded, tap_row, tap_col),
                cot_whole,
                preferred_element_type=jnp.float32,
            )
            block = block.reshape(3, channels, cot_whole.shape[1])
            for tap_depth in range(3):
                pieces[tap_depth * 9 + tap_row * 3 + tap_col] = block[tap_depth]
    return jnp.stack(pieces, axis=0)


def conv_forward(padded, taps):
    planes, channels, cells = padded.shape
    lhs = padded.reshape(1, planes, channels, PLANE_ROWS, ROW_CELLS)
    rhs = taps.reshape(3, 3, 3, channels, taps.shape[-1])
    out = lax.conv_general_dilated(
        lhs, rhs, (1, 1, 1), [(0, 0), (1, 1), (1, 1)],
        dimension_numbers=("NDCHW", "DHWIO", "NDCHW"),
        preferred_element_type=jnp.float32,
    )
    return out.reshape(planes - 2, taps.shape[-1], cells)


def conv_backward(cot_padded, taps):
    planes, channels, cells = cot_padded.shape
    lhs = cot_padded.reshape(1, planes, channels, PLANE_ROWS, ROW_CELLS)
    rhs = taps.reshape(3, 3, 3, taps.shape[1], channels)[::-1, ::-1, ::-1]
    out = lax.conv_general_dilated(
        lhs, rhs, (1, 1, 1), [(0, 0), (1, 1), (1, 1)],
        dimension_numbers=("NDCHW", "DHWOI", "NDCHW"),
        preferred_element_type=jnp.float32,
    )
    return out.reshape(planes - 2, taps.shape[1], cells)


FLAT_EDGE = 128


def filter_kernel(x_ref, c_ref, o_ref):
    cells = c_ref.shape[0]
    width = x_ref.shape[-1]
    column = lax.broadcasted_iota(jnp.int32, (x_ref.shape[1], cells), 1) % ROW_CELLS
    cot = c_ref[...]
    for tap_depth in range(3):
        plane = x_ref[tap_depth].astype(jnp.float32)
        for tap_row in range(3):
            for tap_col in range(3):
                offset = FLAT_EDGE + (tap_row - 1) * ROW_CELLS + (tap_col - 1)
                moved = pltpu.roll(plane, (width - offset) % width, 1)[:, :cells]
                if tap_col == 0:
                    moved = jnp.where(column >= 1, moved, 0.0)
                if tap_col == 2:
                    moved = jnp.where(column < ROW_CELLS - 1, moved, 0.0)
                o_ref[tap_depth * 9 + tap_row * 3 + tap_col] = jnp.dot(
                    moved.astype(jnp.bfloat16), cot, preferred_element_type=jnp.float32
                )


def conv_filter(padded, cot_whole):
    planes, channels, cells = padded.shape
    flat = jnp.pad(padded, ((0, 0), (0, 0), (FLAT_EDGE, FLAT_EDGE)))
    cot_t = cot_whole[0].T
    return pl.pallas_call(
        filter_kernel,
        out_shape=jax.ShapeDtypeStruct((27, channels, cot_t.shape[1]), jnp.float32),
    )(flat, cot_t)


def scatter_sum(block, axis, dim):
    count = lax.axis_size(axis)
    shape = block.shape
    parts = block.reshape(shape[:dim] + (count, shape[dim] // count) + shape[dim + 1 :])
    parts = jnp.moveaxis(parts, dim, 0)
    parts = lax.all_to_all(parts, axis, 0, 0, tiled=True)
    return parts.sum(axis=0)


def spread_gather(block, axis, dim):
    count = lax.axis_size(axis)
    copies = jnp.broadcast_to(block[None], (count,) + block.shape)
    copies = lax.all_to_all(copies, axis, 0, 0, tiled=True)
    copies = jnp.moveaxis(copies, 0, dim)
    shape = block.shape
    return copies.reshape(shape[:dim] + (count * shape[dim],) + shape[dim + 1 :])


def local(inputs, weights, cotangent):
    padded = extended(inputs, (("space", 0),), 1)
    partial_out = conv_forward(padded, weights)
    partial_out, padded = lax.optimization_barrier((partial_out, padded))
    output = scatter_sum(partial_out, "chan", 1).astype(jnp.bfloat16)
    gathered = doubling_gather(cotangent, "chan", partner_masks(lax.axis_size("chan"), 1), 1)
    cot_padded = extended(gathered, (("space", 0),), 1)
    cot_whole = cot_padded[1:-1]
    input_grad = conv_backward(cot_padded, weights).astype(jnp.bfloat16)
    local_terms = conv_filter(padded, cot_whole)
    flat = local_terms.reshape(-1, local_terms.shape[-1])
    flat = spread_gather(scatter_sum(flat, "space", 0), "space", 0)
    weight_grad = flat.reshape(local_terms.shape)
    return (output, input_grad, weight_grad)


def solution(mesh):
    placed = (P("space", "chan", None), P(None, "chan", None), P("space", "chan", None))
    return jax.shard_map(
        local,
        mesh=mesh,
        in_specs=placed,
        out_specs=(P("space", "chan", None), P("space", "chan", None), P(None, "chan", None)),
        check_vma=False,
    )
```

```python
import jax
import jax.numpy as jnp
from jax import lax
from jax.sharding import PartitionSpec as P
from jax.experimental import pallas as pl
from jax.experimental.pallas import tpu as pltpu

PLANE_ROWS = 32
ROW_CELLS = 64


def extended(block, sides, width):
    for axis, dim in sides:
        count = lax.axis_size(axis)
        forward = [(i, i + 1) for i in range(count - 1)]
        backward = [(target, source) for source, target in forward]
        low = lax.ppermute(
            lax.slice_in_dim(block, block.shape[dim] - width, None, axis=dim), axis, forward
        )
        high = lax.ppermute(lax.slice_in_dim(block, 0, width, axis=dim), axis, backward)
        block = jnp.concatenate([low, block, high], axis=dim)
    return block


def partner_masks(count, first):
    masks = [1 << b for b in range(count.bit_length() - 1)]
    return [first] + [m for m in masks if m != first]


def halving_sum(block, axis, masks, dim):
    count = lax.axis_size(axis)
    index = lax.axis_index(axis)
    for mask in masks:
        half = block.shape[dim] // 2
        upper = (index // mask) % 2 == 1
        low = lax.slice_in_dim(block, 0, half, axis=dim)
        high = lax.slice_in_dim(block, half, 2 * half, axis=dim)
        keep = jnp.where(upper, high, low)
        send = jnp.where(upper, low, high)
        block = keep + lax.ppermute(send, axis, [(i, i ^ mask) for i in range(count)])
    return block


def doubling_gather(block, axis, masks, dim):
    count = lax.axis_size(axis)
    index = lax.axis_index(axis)
    for mask in masks:
        upper = (index // mask) % 2 == 1
        other = lax.ppermute(block, axis, [(i, i ^ mask) for i in range(count)])
        block = jnp.concatenate(
            [jnp.where(upper, other, block), jnp.where(upper, block, other)], axis=dim
        )
    return block


def plane_shift(field, tap_row, tap_col):
    lead = field.shape[:-1]
    grid = field.reshape(lead + (PLANE_ROWS, ROW_CELLS))
    padded = jnp.pad(grid, [(0, 0)] * len(lead) + [(1, 1), (1, 1)])
    window = padded[..., tap_row : tap_row + PLANE_ROWS, tap_col : tap_col + ROW_CELLS]
    return window.reshape(lead + (PLANE_ROWS * ROW_CELLS,))


def stack_at(padded, tap_row, tap_col):
    planes = padded.shape[0] - 2
    moved = plane_shift(padded, tap_row, tap_col)
    return jnp.concatenate(
        [moved[tap_depth : tap_depth + planes] for tap_depth in range(3)], axis=1
    )


def tap_weights(taps, tap_row, tap_col):
    return jnp.concatenate(
        [taps[tap_depth * 9 + tap_row * 3 + tap_col] for tap_depth in range(3)], axis=0
    )


def convolve(padded, taps):
    total = None
    for tap_row in range(3):
        for tap_col in range(3):
            term = jnp.einsum(
                "dcp,co->dop",
                stack_at(padded, tap_row, tap_col),
                tap_weights(taps, tap_row, tap_col),
                preferred_element_type=jnp.float32,
            )
            total = term if total is None else total + term
    return total


def weight_terms(padded, cot_whole, channels):
    pieces = [None] * 27
    for tap_row in range(3):
        for tap_col in range(3):
            block = jnp.einsum(
                "dcp,dop->co",
                stack_at(padded, tap_row, tap_col),
                cot_whole,
                preferred_element_type=jnp.float32,
            )
            block = block.reshape(3, channels, cot_whole.shape[1])
            for tap_depth in range(3):
                pieces[tap_depth * 9 + tap_row * 3 + tap_col] = block[tap_depth]
    return jnp.stack(pieces, axis=0)


def conv_forward(padded, taps):
    planes, channels, cells = padded.shape
    lhs = padded.reshape(1, planes, channels, PLANE_ROWS, ROW_CELLS)
    rhs = taps.reshape(3, 3, 3, channels, taps.shape[-1])
    out = lax.conv_general_dilated(
        lhs, rhs, (1, 1, 1), [(0, 0), (1, 1), (1, 1)],
        dimension_numbers=("NDCHW", "DHWIO", "NDCHW"),
        preferred_element_type=jnp.float32,
    )
    return out.reshape(planes - 2, taps.shape[-1], cells)


def conv_backward(cot_padded, taps):
    planes, channels, cells = cot_padded.shape
    lhs = cot_padded.reshape(1, planes, channels, PLANE_ROWS, ROW_CELLS)
    rhs = taps.reshape(3, 3, 3, taps.shape[1], channels)[::-1, ::-1, ::-1]
    out = lax.conv_general_dilated(
        lhs, rhs, (1, 1, 1), [(0, 0), (1, 1), (1, 1)],
        dimension_numbers=("NDCHW", "DHWOI", "NDCHW"),
        preferred_element_type=jnp.float32,
    )
    return out.reshape(planes - 2, taps.shape[1], cells)


FLAT_EDGE = 128


def filter_kernel(x_ref, c_ref, o_ref):
    cells = c_ref.shape[0]
    width = x_ref.shape[-1]
    column = lax.broadcasted_iota(jnp.int32, (x_ref.shape[1], cells), 1) % ROW_CELLS
    cot = c_ref[...]
    for tap_depth in range(3):
        plane = x_ref[tap_depth].astype(jnp.float32)
        for tap_row in range(3):
            for tap_col in range(3):
                offset = FLAT_EDGE + (tap_row - 1) * ROW_CELLS + (tap_col - 1)
                moved = pltpu.roll(plane, (width - offset) % width, 1)[:, :cells]
                if tap_col == 0:
                    moved = jnp.where(column >= 1, moved, 0.0)
                if tap_col == 2:
                    moved = jnp.where(column < ROW_CELLS - 1, moved, 0.0)
                o_ref[tap_depth * 9 + tap_row * 3 + tap_col] = jnp.dot(
                    moved.astype(jnp.bfloat16), cot, preferred_element_type=jnp.float32
                )


def conv_filter(padded, cot_whole):
    planes, channels, cells = padded.shape
    flat = jnp.pad(padded, ((0, 0), (0, 0), (FLAT_EDGE, FLAT_EDGE)))
    cot_t = cot_whole[0].T
    return pl.pallas_call(
        filter_kernel,
        out_shape=jax.ShapeDtypeStruct((27, channels, cot_t.shape[1]), jnp.float32),
    )(flat, cot_t)


def scatter_sum(block, axis, dim):
    count = lax.axis_size(axis)
    shape = block.shape
    parts = block.reshape(shape[:dim] + (count, shape[dim] // count) + shape[dim + 1 :])
    parts = jnp.moveaxis(parts, dim, 0)
    parts = lax.all_to_all(parts, axis, 0, 0, tiled=True)
    return parts.sum(axis=0)


def spread_gather(block, axis, dim):
    count = lax.axis_size(axis)
    copies = jnp.broadcast_to(block[None], (count,) + block.shape)
    copies = lax.all_to_all(copies, axis, 0, 0, tiled=True)
    copies = jnp.moveaxis(copies, 0, dim)
    shape = block.shape
    return copies.reshape(shape[:dim] + (count * shape[dim],) + shape[dim + 1 :])


def local(inputs, weights, cotangent):
    padded = extended(inputs, (("space", 0),), 1)
    partial_out = conv_forward(padded, weights)
    output = scatter_sum(partial_out, "chan", 1).astype(jnp.bfloat16)
    gathered = spread_gather(cotangent, "chan", 1)
    cot_padded = extended(gathered, (("space", 0),), 1)
    cot_whole = cot_padded[1:-1]
    input_grad = conv_backward(cot_padded, weights).astype(jnp.bfloat16)
    local_terms = conv_filter(padded, cot_whole)
    flat = local_terms.reshape(-1, local_terms.shape[-1])
    flat = spread_gather(scatter_sum(flat, "space", 0), "space", 0)
    weight_grad = flat.reshape(local_terms.shape)
    return (output, input_grad, weight_grad)


def solution(mesh):
    placed = (P("space", "chan", None), P(None, "chan", None), P("space", "chan", None))
    return jax.shard_map(
        local,
        mesh=mesh,
        in_specs=placed,
        out_specs=(P("space", "chan", None), P("space", "chan", None), P(None, "chan", None)),
        check_vma=False,
    )
```

```python
import jax
import jax.numpy as jnp
from jax import lax
from jax.sharding import PartitionSpec as P
from jax.experimental import pallas as pl
from jax.experimental.pallas import tpu as pltpu

PLANE_ROWS = 32
ROW_CELLS = 64


def extended(block, sides, width):
    for axis, dim in sides:
        count = lax.axis_size(axis)
        forward = [(i, i + 1) for i in range(count - 1)]
        backward = [(target, source) for source, target in forward]
        low = lax.ppermute(
            lax.slice_in_dim(block, block.shape[dim] - width, None, axis=dim), axis, forward
        )
        high = lax.ppermute(lax.slice_in_dim(block, 0, width, axis=dim), axis, backward)
        block = jnp.concatenate([low, block, high], axis=dim)
    return block


def partner_masks(count, first):
    masks = [1 << b for b in range(count.bit_length() - 1)]
    return [first] + [m for m in masks if m != first]


def halving_sum(block, axis, masks, dim):
    count = lax.axis_size(axis)
    index = lax.axis_index(axis)
    for mask in masks:
        half = block.shape[dim] // 2
        upper = (index // mask) % 2 == 1
        low = lax.slice_in_dim(block, 0, half, axis=dim)
        high = lax.slice_in_dim(block, half, 2 * half, axis=dim)
        keep = jnp.where(upper, high, low)
        send = jnp.where(upper, low, high)
        block = keep + lax.ppermute(send, axis, [(i, i ^ mask) for i in range(count)])
    return block


def doubling_gather(block, axis, masks, dim):
    count = lax.axis_size(axis)
    index = lax.axis_index(axis)
    for mask in masks:
        upper = (index // mask) % 2 == 1
        other = lax.ppermute(block, axis, [(i, i ^ mask) for i in range(count)])
        block = jnp.concatenate(
            [jnp.where(upper, other, block), jnp.where(upper, block, other)], axis=dim
        )
    return block


def plane_shift(field, tap_row, tap_col):
    lead = field.shape[:-1]
    grid = field.reshape(lead + (PLANE_ROWS, ROW_CELLS))
    padded = jnp.pad(grid, [(0, 0)] * len(lead) + [(1, 1), (1, 1)])
    window = padded[..., tap_row : tap_row + PLANE_ROWS, tap_col : tap_col + ROW_CELLS]
    return window.reshape(lead + (PLANE_ROWS * ROW_CELLS,))


def stack_at(padded, tap_row, tap_col):
    planes = padded.shape[0] - 2
    moved = plane_shift(padded, tap_row, tap_col)
    return jnp.concatenate(
        [moved[tap_depth : tap_depth + planes] for tap_depth in range(3)], axis=1
    )


def tap_weights(taps, tap_row, tap_col):
    return jnp.concatenate(
        [taps[tap_depth * 9 + tap_row * 3 + tap_col] for tap_depth in range(3)], axis=0
    )


def convolve(padded, taps):
    total = None
    for tap_row in range(3):
        for tap_col in range(3):
            term = jnp.einsum(
                "dcp,co->dop",
                stack_at(padded, tap_row, tap_col),
                tap_weights(taps, tap_row, tap_col),
                preferred_element_type=jnp.float32,
            )
            total = term if total is None else total + term
    return total


def weight_terms(padded, cot_whole, channels):
    pieces = [None] * 27
    for tap_row in range(3):
        for tap_col in range(3):
            block = jnp.einsum(
                "dcp,dop->co",
                stack_at(padded, tap_row, tap_col),
                cot_whole,
                preferred_element_type=jnp.float32,
            )
            block = block.reshape(3, channels, cot_whole.shape[1])
            for tap_depth in range(3):
                pieces[tap_depth * 9 + tap_row * 3 + tap_col] = block[tap_depth]
    return jnp.stack(pieces, axis=0)


def conv_forward(padded, taps):
    planes, channels, cells = padded.shape
    lhs = padded.reshape(1, planes, channels, PLANE_ROWS, ROW_CELLS)
    rhs = taps.reshape(3, 3, 3, channels, taps.shape[-1])
    out = lax.conv_general_dilated(
        lhs, rhs, (1, 1, 1), [(0, 0), (1, 1), (1, 1)],
        dimension_numbers=("NDCHW", "DHWIO", "NDCHW"),
        preferred_element_type=jnp.float32,
    )
    return out.reshape(planes - 2, taps.shape[-1], cells)


def conv_backward(cot_plane, taps):
    planes, channels, cells = cot_plane.shape
    lhs = cot_plane.reshape(1, planes, channels, PLANE_ROWS, ROW_CELLS)
    rhs = taps.reshape(3, 3, 3, taps.shape[1], channels)[::-1, ::-1, ::-1]
    out = lax.conv_general_dilated(
        lhs, rhs, (1, 1, 1), [(2, 2), (1, 1), (1, 1)],
        dimension_numbers=("NDCHW", "DHWOI", "NDCHW"),
        preferred_element_type=jnp.float32,
    )
    return out.reshape(planes + 2, taps.shape[1], cells)


def spill_sum(parts, axis):
    count = lax.axis_size(axis)
    forward = [(i, i + 1) for i in range(count - 1)]
    backward = [(target, source) for source, target in forward]
    from_low = lax.ppermute(parts[-1:], axis, forward)
    from_high = lax.ppermute(parts[:1], axis, backward)
    return parts[1:-1] + from_low + from_high


FLAT_EDGE = 128


def filter_kernel(x_ref, c_ref, o_ref):
    cells = c_ref.shape[0]
    width = x_ref.shape[-1]
    column = lax.broadcasted_iota(jnp.int32, (x_ref.shape[1], cells), 1) % ROW_CELLS
    cot = c_ref[...]
    for tap_depth in range(3):
        plane = x_ref[tap_depth].astype(jnp.float32)
        for tap_row in range(3):
            for tap_col in range(3):
                offset = FLAT_EDGE + (tap_row - 1) * ROW_CELLS + (tap_col - 1)
                moved = pltpu.roll(plane, (width - offset) % width, 1)[:, :cells]
                if tap_col == 0:
                    moved = jnp.where(column >= 1, moved, 0.0)
                if tap_col == 2:
                    moved = jnp.where(column < ROW_CELLS - 1, moved, 0.0)
                o_ref[tap_depth * 9 + tap_row * 3 + tap_col] = jnp.dot(
                    moved.astype(jnp.bfloat16), cot, preferred_element_type=jnp.float32
                )


def conv_filter(padded, cot_whole):
    planes, channels, cells = padded.shape
    flat = jnp.pad(padded, ((0, 0), (0, 0), (FLAT_EDGE, FLAT_EDGE)))
    cot_t = cot_whole[0].T
    return pl.pallas_call(
        filter_kernel,
        out_shape=jax.ShapeDtypeStruct((27, channels, cot_t.shape[1]), jnp.float32),
    )(flat, cot_t)


def scatter_sum(block, axis, dim):
    count = lax.axis_size(axis)
    shape = block.shape
    parts = block.reshape(shape[:dim] + (count, shape[dim] // count) + shape[dim + 1 :])
    parts = jnp.moveaxis(parts, dim, 0)
    parts = lax.all_to_all(parts, axis, 0, 0, tiled=True)
    return parts.sum(axis=0)


def spread_gather(block, axis, dim):
    count = lax.axis_size(axis)
    copies = jnp.broadcast_to(block[None], (count,) + block.shape)
    copies = lax.all_to_all(copies, axis, 0, 0, tiled=True)
    copies = jnp.moveaxis(copies, 0, dim)
    shape = block.shape
    return copies.reshape(shape[:dim] + (count * shape[dim],) + shape[dim + 1 :])


def local(inputs, weights, cotangent):
    padded = extended(inputs, (("space", 0),), 1)
    partial_out = conv_forward(padded, weights)
    output = scatter_sum(partial_out, "chan", 1).astype(jnp.bfloat16)
    gathered = spread_gather(cotangent, "chan", 1)
    input_grad = spill_sum(conv_backward(gathered, weights), "space").astype(jnp.bfloat16)
    local_terms = conv_filter(padded, gathered)
    flat = local_terms.reshape(-1, local_terms.shape[-1])
    flat = spread_gather(scatter_sum(flat, "space", 0), "space", 0)
    weight_grad = flat.reshape(local_terms.shape)
    return (output, input_grad, weight_grad)


def solution(mesh):
    placed = (P("space", "chan", None), P(None, "chan", None), P("space", "chan", None))
    return jax.shard_map(
        local,
        mesh=mesh,
        in_specs=placed,
        out_specs=(P("space", "chan", None), P("space", "chan", None), P(None, "chan", None)),
        check_vma=False,
    )
```

```python
import jax
import jax.numpy as jnp
from jax import lax
from jax.sharding import PartitionSpec as P
from jax.experimental import pallas as pl
from jax.experimental.pallas import tpu as pltpu

PLANE_ROWS = 32
ROW_CELLS = 64


def extended(block, sides, width):
    for axis, dim in sides:
        count = lax.axis_size(axis)
        forward = [(i, i + 1) for i in range(count - 1)]
        backward = [(target, source) for source, target in forward]
        low = lax.ppermute(
            lax.slice_in_dim(block, block.shape[dim] - width, None, axis=dim), axis, forward
        )
        high = lax.ppermute(lax.slice_in_dim(block, 0, width, axis=dim), axis, backward)
        block = jnp.concatenate([low, block, high], axis=dim)
    return block


def partner_masks(count, first):
    masks = [1 << b for b in range(count.bit_length() - 1)]
    return [first] + [m for m in masks if m != first]


def halving_sum(block, axis, masks, dim):
    count = lax.axis_size(axis)
    index = lax.axis_index(axis)
    for mask in masks:
        half = block.shape[dim] // 2
        upper = (index // mask) % 2 == 1
        low = lax.slice_in_dim(block, 0, half, axis=dim)
        high = lax.slice_in_dim(block, half, 2 * half, axis=dim)
        keep = jnp.where(upper, high, low)
        send = jnp.where(upper, low, high)
        block = keep + lax.ppermute(send, axis, [(i, i ^ mask) for i in range(count)])
    return block


def doubling_gather(block, axis, masks, dim):
    count = lax.axis_size(axis)
    index = lax.axis_index(axis)
    for mask in masks:
        upper = (index // mask) % 2 == 1
        other = lax.ppermute(block, axis, [(i, i ^ mask) for i in range(count)])
        block = jnp.concatenate(
            [jnp.where(upper, other, block), jnp.where(upper, block, other)], axis=dim
        )
    return block


def plane_shift(field, tap_row, tap_col):
    lead = field.shape[:-1]
    grid = field.reshape(lead + (PLANE_ROWS, ROW_CELLS))
    padded = jnp.pad(grid, [(0, 0)] * len(lead) + [(1, 1), (1, 1)])
    window = padded[..., tap_row : tap_row + PLANE_ROWS, tap_col : tap_col + ROW_CELLS]
    return window.reshape(lead + (PLANE_ROWS * ROW_CELLS,))


def stack_at(padded, tap_row, tap_col):
    planes = padded.shape[0] - 2
    moved = plane_shift(padded, tap_row, tap_col)
    return jnp.concatenate(
        [moved[tap_depth : tap_depth + planes] for tap_depth in range(3)], axis=1
    )


def tap_weights(taps, tap_row, tap_col):
    return jnp.concatenate(
        [taps[tap_depth * 9 + tap_row * 3 + tap_col] for tap_depth in range(3)], axis=0
    )


def convolve(padded, taps):
    total = None
    for tap_row in range(3):
        for tap_col in range(3):
            term = jnp.einsum(
                "dcp,co->dop",
                stack_at(padded, tap_row, tap_col),
                tap_weights(taps, tap_row, tap_col),
                preferred_element_type=jnp.float32,
            )
            total = term if total is None else total + term
    return total


def weight_terms(padded, cot_whole, channels):
    pieces = [None] * 27
    for tap_row in range(3):
        for tap_col in range(3):
            block = jnp.einsum(
                "dcp,dop->co",
                stack_at(padded, tap_row, tap_col),
                cot_whole,
                preferred_element_type=jnp.float32,
            )
            block = block.reshape(3, channels, cot_whole.shape[1])
            for tap_depth in range(3):
                pieces[tap_depth * 9 + tap_row * 3 + tap_col] = block[tap_depth]
    return jnp.stack(pieces, axis=0)


def conv_forward(padded, taps):
    planes, channels, cells = padded.shape
    lhs = padded.reshape(1, planes, channels, PLANE_ROWS, ROW_CELLS)
    rhs = taps.reshape(3, 3, 3, channels, taps.shape[-1])
    out = lax.conv_general_dilated(
        lhs, rhs, (1, 1, 1), [(0, 0), (1, 1), (1, 1)],
        dimension_numbers=("NDCHW", "DHWIO", "NDCHW"),
        preferred_element_type=jnp.float32,
    )
    return out.reshape(planes - 2, taps.shape[-1], cells)


def conv_backward(cot_plane, taps):
    planes, channels, cells = cot_plane.shape
    lhs = cot_plane.reshape(1, planes, channels, PLANE_ROWS, ROW_CELLS)
    rhs = taps.reshape(3, 3, 3, taps.shape[1], channels)[::-1, ::-1, ::-1]
    out = lax.conv_general_dilated(
        lhs, rhs, (1, 1, 1), [(2, 2), (1, 1), (1, 1)],
        dimension_numbers=("NDCHW", "DHWOI", "NDCHW"),
        preferred_element_type=jnp.float32,
    )
    return out.reshape(planes + 2, taps.shape[1], cells)


def spill_sum(parts, axis):
    count = lax.axis_size(axis)
    forward = [(i, i + 1) for i in range(count - 1)]
    backward = [(target, source) for source, target in forward]
    from_low = lax.ppermute(parts[-1:], axis, forward)
    from_high = lax.ppermute(parts[:1], axis, backward)
    return parts[1:-1] + from_low + from_high


FLAT_EDGE = 128


def filter_kernel(x_ref, c_ref, o_ref):
    cells = c_ref.shape[0]
    width = x_ref.shape[-1]
    column = lax.broadcasted_iota(jnp.int32, (x_ref.shape[1], cells), 1) % ROW_CELLS
    cot = c_ref[...]
    for tap_depth in range(3):
        plane = x_ref[tap_depth].astype(jnp.float32)
        for tap_row in range(3):
            for tap_col in range(3):
                offset = FLAT_EDGE + (tap_row - 1) * ROW_CELLS + (tap_col - 1)
                moved = pltpu.roll(plane, (width - offset) % width, 1)[:, :cells]
                if tap_col == 0:
                    moved = jnp.where(column >= 1, moved, 0.0)
                if tap_col == 2:
                    moved = jnp.where(column < ROW_CELLS - 1, moved, 0.0)
                o_ref[tap_depth * 9 + tap_row * 3 + tap_col] = jnp.dot(
                    moved.astype(jnp.bfloat16), cot, preferred_element_type=jnp.float32
                )


def conv_filter(padded, cot_whole):
    planes, channels, cells = padded.shape
    flat = jnp.pad(padded, ((0, 0), (0, 0), (FLAT_EDGE, FLAT_EDGE)))
    cot_t = cot_whole[0].T
    return pl.pallas_call(
        filter_kernel,
        out_shape=jax.ShapeDtypeStruct((27, channels, cot_t.shape[1]), jnp.float32),
    )(flat, cot_t)


def scatter_sum(block, axis, dim):
    count = lax.axis_size(axis)
    shape = block.shape
    parts = block.reshape(shape[:dim] + (count, shape[dim] // count) + shape[dim + 1 :])
    parts = jnp.moveaxis(parts, dim, 0)
    parts = lax.all_to_all(parts, axis, 0, 0, tiled=True)
    return parts.sum(axis=0)


def spread_gather(block, axis, dim):
    count = lax.axis_size(axis)
    copies = jnp.broadcast_to(block[None], (count,) + block.shape)
    copies = lax.all_to_all(copies, axis, 0, 0, tiled=True)
    copies = jnp.moveaxis(copies, 0, dim)
    shape = block.shape
    return copies.reshape(shape[:dim] + (count * shape[dim],) + shape[dim + 1 :])


def local(inputs, weights, cotangent):
    padded = extended(inputs, (("space", 0),), 1)
    partial_out = conv_forward(padded, weights)
    chan_masks = partner_masks(lax.axis_size("chan"), 1)[::-1]
    output = halving_sum(partial_out, "chan", chan_masks, 1).astype(jnp.bfloat16)
    gathered = spread_gather(cotangent, "chan", 1)
    input_grad = spill_sum(conv_backward(gathered, weights), "space").astype(jnp.bfloat16)
    local_terms = conv_filter(padded, gathered)
    flat = local_terms.reshape(-1, local_terms.shape[-1])
    flat = spread_gather(scatter_sum(flat, "space", 0), "space", 0)
    weight_grad = flat.reshape(local_terms.shape)
    return (output, input_grad, weight_grad)


def solution(mesh):
    placed = (P("space", "chan", None), P(None, "chan", None), P("space", "chan", None))
    return jax.shard_map(
        local,
        mesh=mesh,
        in_specs=placed,
        out_specs=(P("space", "chan", None), P("space", "chan", None), P(None, "chan", None)),
        check_vma=False,
    )
```

```python
import jax
import jax.numpy as jnp
from jax import lax
from jax.sharding import PartitionSpec as P
from jax.experimental import pallas as pl
from jax.experimental.pallas import tpu as pltpu

PLANE_ROWS = 32
ROW_CELLS = 64


def extended(block, sides, width):
    for axis, dim in sides:
        count = lax.axis_size(axis)
        forward = [(i, i + 1) for i in range(count - 1)]
        backward = [(target, source) for source, target in forward]
        low = lax.ppermute(
            lax.slice_in_dim(block, block.shape[dim] - width, None, axis=dim), axis, forward
        )
        high = lax.ppermute(lax.slice_in_dim(block, 0, width, axis=dim), axis, backward)
        block = jnp.concatenate([low, block, high], axis=dim)
    return block


def partner_masks(count, first):
    masks = [1 << b for b in range(count.bit_length() - 1)]
    return [first] + [m for m in masks if m != first]


def halving_sum(block, axis, masks, dim):
    count = lax.axis_size(axis)
    index = lax.axis_index(axis)
    for mask in masks:
        half = block.shape[dim] // 2
        upper = (index // mask) % 2 == 1
        low = lax.slice_in_dim(block, 0, half, axis=dim)
        high = lax.slice_in_dim(block, half, 2 * half, axis=dim)
        keep = jnp.where(upper, high, low)
        send = jnp.where(upper, low, high)
        block = keep + lax.ppermute(send, axis, [(i, i ^ mask) for i in range(count)])
    return block


def doubling_gather(block, axis, masks, dim):
    count = lax.axis_size(axis)
    index = lax.axis_index(axis)
    for mask in masks:
        upper = (index // mask) % 2 == 1
        other = lax.ppermute(block, axis, [(i, i ^ mask) for i in range(count)])
        block = jnp.concatenate(
            [jnp.where(upper, other, block), jnp.where(upper, block, other)], axis=dim
        )
    return block


def plane_shift(field, tap_row, tap_col):
    lead = field.shape[:-1]
    grid = field.reshape(lead + (PLANE_ROWS, ROW_CELLS))
    padded = jnp.pad(grid, [(0, 0)] * len(lead) + [(1, 1), (1, 1)])
    window = padded[..., tap_row : tap_row + PLANE_ROWS, tap_col : tap_col + ROW_CELLS]
    return window.reshape(lead + (PLANE_ROWS * ROW_CELLS,))


def stack_at(padded, tap_row, tap_col):
    planes = padded.shape[0] - 2
    moved = plane_shift(padded, tap_row, tap_col)
    return jnp.concatenate(
        [moved[tap_depth : tap_depth + planes] for tap_depth in range(3)], axis=1
    )


def tap_weights(taps, tap_row, tap_col):
    return jnp.concatenate(
        [taps[tap_depth * 9 + tap_row * 3 + tap_col] for tap_depth in range(3)], axis=0
    )


def convolve(padded, taps):
    total = None
    for tap_row in range(3):
        for tap_col in range(3):
            term = jnp.einsum(
                "dcp,co->dop",
                stack_at(padded, tap_row, tap_col),
                tap_weights(taps, tap_row, tap_col),
                preferred_element_type=jnp.float32,
            )
            total = term if total is None else total + term
    return total


def weight_terms(padded, cot_whole, channels):
    pieces = [None] * 27
    for tap_row in range(3):
        for tap_col in range(3):
            block = jnp.einsum(
                "dcp,dop->co",
                stack_at(padded, tap_row, tap_col),
                cot_whole,
                preferred_element_type=jnp.float32,
            )
            block = block.reshape(3, channels, cot_whole.shape[1])
            for tap_depth in range(3):
                pieces[tap_depth * 9 + tap_row * 3 + tap_col] = block[tap_depth]
    return jnp.stack(pieces, axis=0)


def conv_forward(padded, taps):
    planes, channels, cells = padded.shape
    lhs = padded.reshape(1, planes, channels, PLANE_ROWS, ROW_CELLS)
    rhs = taps.reshape(3, 3, 3, channels, taps.shape[-1])
    out = lax.conv_general_dilated(
        lhs, rhs, (1, 1, 1), [(0, 0), (1, 1), (1, 1)],
        dimension_numbers=("NDCHW", "DHWIO", "NDCHW"),
        preferred_element_type=jnp.float32,
    )
    return out.reshape(planes - 2, taps.shape[-1], cells)


def conv_backward(cot_plane, taps):
    planes, channels, cells = cot_plane.shape
    lhs = cot_plane.reshape(1, planes, channels, PLANE_ROWS, ROW_CELLS)
    rhs = taps.reshape(3, 3, 3, taps.shape[1], channels)[::-1, ::-1, ::-1]
    out = lax.conv_general_dilated(
        lhs, rhs, (1, 1, 1), [(2, 2), (1, 1), (1, 1)],
        dimension_numbers=("NDCHW", "DHWOI", "NDCHW"),
        preferred_element_type=jnp.float32,
    )
    return out.reshape(planes + 2, taps.shape[1], cells)


def spill_sum(parts, axis):
    count = lax.axis_size(axis)
    forward = [(i, i + 1) for i in range(count - 1)]
    backward = [(target, source) for source, target in forward]
    from_low = lax.ppermute(parts[-1:], axis, forward)
    from_high = lax.ppermute(parts[:1], axis, backward)
    return parts[1:-1] + from_low + from_high


FLAT_EDGE = 128


def filter_kernel(x_ref, c_ref, o_ref):
    cells = c_ref.shape[0]
    width = x_ref.shape[-1]
    column = lax.broadcasted_iota(jnp.int32, (x_ref.shape[1], cells), 1) % ROW_CELLS
    cot = c_ref[...]
    for tap_depth in range(3):
        plane = x_ref[tap_depth].astype(jnp.float32)
        for tap_row in range(3):
            for tap_col in range(3):
                offset = FLAT_EDGE + (tap_row - 1) * ROW_CELLS + (tap_col - 1)
                moved = pltpu.roll(plane, (width - offset) % width, 1)[:, :cells]
                if tap_col == 0:
                    moved = jnp.where(column >= 1, moved, 0.0)
                if tap_col == 2:
                    moved = jnp.where(column < ROW_CELLS - 1, moved, 0.0)
                o_ref[tap_depth * 9 + tap_row * 3 + tap_col] = jnp.dot(
                    moved.astype(jnp.bfloat16), cot, preferred_element_type=jnp.float32
                )


def conv_filter(padded, cot_whole):
    planes, channels, cells = padded.shape
    flat = jnp.pad(padded, ((0, 0), (0, 0), (FLAT_EDGE, FLAT_EDGE)))
    cot_t = cot_whole[0].T
    return pl.pallas_call(
        filter_kernel,
        out_shape=jax.ShapeDtypeStruct((27, channels, cot_t.shape[1]), jnp.float32),
    )(flat, cot_t)


def scatter_sum(block, axis, dim):
    count = lax.axis_size(axis)
    shape = block.shape
    parts = block.reshape(shape[:dim] + (count, shape[dim] // count) + shape[dim + 1 :])
    parts = jnp.moveaxis(parts, dim, 0)
    parts = lax.all_to_all(parts, axis, 0, 0, tiled=True)
    return parts.sum(axis=0)


def spread_gather(block, axis, dim):
    count = lax.axis_size(axis)
    copies = jnp.broadcast_to(block[None], (count,) + block.shape)
    copies = lax.all_to_all(copies, axis, 0, 0, tiled=True)
    copies = jnp.moveaxis(copies, 0, dim)
    shape = block.shape
    return copies.reshape(shape[:dim] + (count * shape[dim],) + shape[dim + 1 :])


SPACE = ("srest", "core")


def local(inputs, weights, cotangent):
    padded = extended(inputs, ((SPACE, 0),), 1)
    partial_out = conv_forward(padded, weights)
    chan_masks = partner_masks(lax.axis_size("chan"), 1)[::-1]
    output = halving_sum(partial_out, "chan", chan_masks, 1).astype(jnp.bfloat16)
    gathered = spread_gather(cotangent, "chan", 1)
    input_grad = spill_sum(conv_backward(gathered, weights), SPACE).astype(jnp.bfloat16)
    local_terms = conv_filter(padded, gathered)
    flat = local_terms.reshape(-1, local_terms.shape[-1])
    flat = halving_sum(flat, "core", [1], 0)
    flat = spread_gather(scatter_sum(flat, "srest", 0), "srest", 0)
    flat = doubling_gather(flat, "core", [1], 0)
    weight_grad = flat.reshape(local_terms.shape)
    return (output, input_grad, weight_grad)


def solution(mesh):
    space, chan = mesh.devices.shape
    split = jax.sharding.Mesh(mesh.devices.reshape(space // 2, 2, chan), SPACE + ("chan",))
    placed = (P(SPACE, "chan", None), P(None, "chan", None), P(SPACE, "chan", None))
    return jax.shard_map(
        local,
        mesh=split,
        in_specs=placed,
        out_specs=(P(SPACE, "chan", None), P(SPACE, "chan", None), P(None, "chan", None)),
        check_vma=False,
    )
```

```python
import jax
import jax.numpy as jnp
from jax import lax
from jax.sharding import PartitionSpec as P
from jax.experimental import pallas as pl
from jax.experimental.pallas import tpu as pltpu

PLANE_ROWS = 32
ROW_CELLS = 64


def extended(block, sides, width):
    for axis, dim in sides:
        count = lax.axis_size(axis)
        forward = [(i, i + 1) for i in range(count - 1)]
        backward = [(target, source) for source, target in forward]
        low = lax.ppermute(
            lax.slice_in_dim(block, block.shape[dim] - width, None, axis=dim), axis, forward
        )
        high = lax.ppermute(lax.slice_in_dim(block, 0, width, axis=dim), axis, backward)
        block = jnp.concatenate([low, block, high], axis=dim)
    return block


def partner_masks(count, first):
    masks = [1 << b for b in range(count.bit_length() - 1)]
    return [first] + [m for m in masks if m != first]


def halving_sum(block, axis, masks, dim):
    count = lax.axis_size(axis)
    index = lax.axis_index(axis)
    for mask in masks:
        half = block.shape[dim] // 2
        upper = (index // mask) % 2 == 1
        low = lax.slice_in_dim(block, 0, half, axis=dim)
        high = lax.slice_in_dim(block, half, 2 * half, axis=dim)
        keep = jnp.where(upper, high, low)
        send = jnp.where(upper, low, high)
        block = keep + lax.ppermute(send, axis, [(i, i ^ mask) for i in range(count)])
    return block


def direct_sum(block, axis, dim):
    count = lax.axis_size(axis)
    index = lax.axis_index(axis)
    width = block.shape[dim] // count
    total = lax.dynamic_slice_in_dim(block, index * width, width, axis=dim)
    for step in range(1, count):
        send = lax.dynamic_slice_in_dim(block, (index ^ step) * width, width, axis=dim)
        total = total + lax.ppermute(send, axis, [(i, i ^ step) for i in range(count)])
    return total


def doubling_gather(block, axis, masks, dim):
    count = lax.axis_size(axis)
    index = lax.axis_index(axis)
    for mask in masks:
        upper = (index // mask) % 2 == 1
        other = lax.ppermute(block, axis, [(i, i ^ mask) for i in range(count)])
        block = jnp.concatenate(
            [jnp.where(upper, other, block), jnp.where(upper, block, other)], axis=dim
        )
    return block


def plane_shift(field, tap_row, tap_col):
    lead = field.shape[:-1]
    grid = field.reshape(lead + (PLANE_ROWS, ROW_CELLS))
    padded = jnp.pad(grid, [(0, 0)] * len(lead) + [(1, 1), (1, 1)])
    window = padded[..., tap_row : tap_row + PLANE_ROWS, tap_col : tap_col + ROW_CELLS]
    return window.reshape(lead + (PLANE_ROWS * ROW_CELLS,))


def stack_at(padded, tap_row, tap_col):
    planes = padded.shape[0] - 2
    moved = plane_shift(padded, tap_row, tap_col)
    return jnp.concatenate(
        [moved[tap_depth : tap_depth + planes] for tap_depth in range(3)], axis=1
    )


def tap_weights(taps, tap_row, tap_col):
    return jnp.concatenate(
        [taps[tap_depth * 9 + tap_row * 3 + tap_col] for tap_depth in range(3)], axis=0
    )


def convolve(padded, taps):
    total = None
    for tap_row in range(3):
        for tap_col in range(3):
            term = jnp.einsum(
                "dcp,co->dop",
                stack_at(padded, tap_row, tap_col),
                tap_weights(taps, tap_row, tap_col),
                preferred_element_type=jnp.float32,
            )
            total = term if total is None else total + term
    return total


def weight_terms(padded, cot_whole, channels):
    pieces = [None] * 27
    for tap_row in range(3):
        for tap_col in range(3):
            block = jnp.einsum(
                "dcp,dop->co",
                stack_at(padded, tap_row, tap_col),
                cot_whole,
                preferred_element_type=jnp.float32,
            )
            block = block.reshape(3, channels, cot_whole.shape[1])
            for tap_depth in range(3):
                pieces[tap_depth * 9 + tap_row * 3 + tap_col] = block[tap_depth]
    return jnp.stack(pieces, axis=0)


def conv_forward(padded, taps):
    planes, channels, cells = padded.shape
    lhs = padded.reshape(1, planes, channels, PLANE_ROWS, ROW_CELLS)
    rhs = taps.reshape(3, 3, 3, channels, taps.shape[-1])
    out = lax.conv_general_dilated(
        lhs, rhs, (1, 1, 1), [(0, 0), (1, 1), (1, 1)],
        dimension_numbers=("NDCHW", "DHWIO", "NDCHW"),
        preferred_element_type=jnp.float32,
    )
    return out.reshape(planes - 2, taps.shape[-1], cells)


def conv_backward(cot_plane, taps):
    planes, channels, cells = cot_plane.shape
    lhs = cot_plane.reshape(1, planes, channels, PLANE_ROWS, ROW_CELLS)
    rhs = taps.reshape(3, 3, 3, taps.shape[1], channels)[::-1, ::-1, ::-1]
    out = lax.conv_general_dilated(
        lhs, rhs, (1, 1, 1), [(2, 2), (1, 1), (1, 1)],
        dimension_numbers=("NDCHW", "DHWOI", "NDCHW"),
        preferred_element_type=jnp.float32,
    )
    return out.reshape(planes + 2, taps.shape[1], cells)


def spill_sum(parts, axis):
    count = lax.axis_size(axis)
    forward = [(i, i + 1) for i in range(count - 1)]
    backward = [(target, source) for source, target in forward]
    from_low = lax.ppermute(parts[-1:], axis, forward)
    from_high = lax.ppermute(parts[:1], axis, backward)
    return parts[1:-1] + from_low + from_high


FLAT_EDGE = 128


def filter_kernel(x_ref, c_ref, o_ref):
    cells = c_ref.shape[0]
    width = x_ref.shape[-1]
    column = lax.broadcasted_iota(jnp.int32, (x_ref.shape[1], cells), 1) % ROW_CELLS
    cot = c_ref[...]
    for tap_depth in range(3):
        plane = x_ref[tap_depth].astype(jnp.float32)
        for tap_row in range(3):
            for tap_col in range(3):
                offset = FLAT_EDGE + (tap_row - 1) * ROW_CELLS + (tap_col - 1)
                moved = pltpu.roll(plane, (width - offset) % width, 1)[:, :cells]
                if tap_col == 0:
                    moved = jnp.where(column >= 1, moved, 0.0)
                if tap_col == 2:
                    moved = jnp.where(column < ROW_CELLS - 1, moved, 0.0)
                o_ref[tap_depth * 9 + tap_row * 3 + tap_col] = jnp.dot(
                    moved.astype(jnp.bfloat16), cot, preferred_element_type=jnp.float32
                )


def conv_filter(padded, cot_whole):
    planes, channels, cells = padded.shape
    flat = jnp.pad(padded, ((0, 0), (0, 0), (FLAT_EDGE, FLAT_EDGE)))
    cot_t = cot_whole[0].T
    return pl.pallas_call(
        filter_kernel,
        out_shape=jax.ShapeDtypeStruct((27, channels, cot_t.shape[1]), jnp.float32),
    )(flat, cot_t)


def scatter_sum(block, axis, dim):
    count = lax.axis_size(axis)
    shape = block.shape
    parts = block.reshape(shape[:dim] + (count, shape[dim] // count) + shape[dim + 1 :])
    parts = jnp.moveaxis(parts, dim, 0)
    parts = lax.all_to_all(parts, axis, 0, 0, tiled=True)
    return parts.sum(axis=0)


def spread_gather(block, axis, dim):
    count = lax.axis_size(axis)
    copies = jnp.broadcast_to(block[None], (count,) + block.shape)
    copies = lax.all_to_all(copies, axis, 0, 0, tiled=True)
    copies = jnp.moveaxis(copies, 0, dim)
    shape = block.shape
    return copies.reshape(shape[:dim] + (count * shape[dim],) + shape[dim + 1 :])


SPACE = ("srest", "core")


def local(inputs, weights, cotangent):
    padded = extended(inputs, ((SPACE, 0),), 1)
    partial_out = conv_forward(padded, weights)
    output = direct_sum(partial_out, "chan", 1).astype(jnp.bfloat16)
    gathered = spread_gather(cotangent, "chan", 1)
    input_grad = spill_sum(conv_backward(gathered, weights), SPACE).astype(jnp.bfloat16)
    local_terms = conv_filter(padded, gathered)
    flat = local_terms.reshape(-1, local_terms.shape[-1])
    flat = halving_sum(flat, "core", [1], 0)
    flat = spread_gather(scatter_sum(flat, "srest", 0), "srest", 0)
    flat = doubling_gather(flat, "core", [1], 0)
    weight_grad = flat.reshape(local_terms.shape)
    return (output, input_grad, weight_grad)


def solution(mesh):
    space, chan = mesh.devices.shape
    split = jax.sharding.Mesh(mesh.devices.reshape(space // 2, 2, chan), SPACE + ("chan",))
    placed = (P(SPACE, "chan", None), P(None, "chan", None), P(SPACE, "chan", None))
    return jax.shard_map(
        local,
        mesh=split,
        in_specs=placed,
        out_specs=(P(SPACE, "chan", None), P(SPACE, "chan", None), P(None, "chan", None)),
        check_vma=False,
    )
```

```python
import jax
import jax.numpy as jnp
from jax import lax
from jax.sharding import PartitionSpec as P
from jax.experimental import pallas as pl
from jax.experimental.pallas import tpu as pltpu

PLANE_ROWS = 32
ROW_CELLS = 64


def extended(block, sides, width):
    for axis, dim in sides:
        count = lax.axis_size(axis)
        forward = [(i, i + 1) for i in range(count - 1)]
        backward = [(target, source) for source, target in forward]
        low = lax.ppermute(
            lax.slice_in_dim(block, block.shape[dim] - width, None, axis=dim), axis, forward
        )
        high = lax.ppermute(lax.slice_in_dim(block, 0, width, axis=dim), axis, backward)
        block = jnp.concatenate([low, block, high], axis=dim)
    return block


def partner_masks(count, first):
    masks = [1 << b for b in range(count.bit_length() - 1)]
    return [first] + [m for m in masks if m != first]


def halving_sum(block, axis, masks, dim):
    count = lax.axis_size(axis)
    index = lax.axis_index(axis)
    for mask in masks:
        half = block.shape[dim] // 2
        upper = (index // mask) % 2 == 1
        low = lax.slice_in_dim(block, 0, half, axis=dim)
        high = lax.slice_in_dim(block, half, 2 * half, axis=dim)
        keep = jnp.where(upper, high, low)
        send = jnp.where(upper, low, high)
        block = keep + lax.ppermute(send, axis, [(i, i ^ mask) for i in range(count)])
    return block


def doubling_gather(block, axis, masks, dim):
    count = lax.axis_size(axis)
    index = lax.axis_index(axis)
    for mask in masks:
        upper = (index // mask) % 2 == 1
        other = lax.ppermute(block, axis, [(i, i ^ mask) for i in range(count)])
        block = jnp.concatenate(
            [jnp.where(upper, other, block), jnp.where(upper, block, other)], axis=dim
        )
    return block


def plane_shift(field, tap_row, tap_col):
    lead = field.shape[:-1]
    grid = field.reshape(lead + (PLANE_ROWS, ROW_CELLS))
    padded = jnp.pad(grid, [(0, 0)] * len(lead) + [(1, 1), (1, 1)])
    window = padded[..., tap_row : tap_row + PLANE_ROWS, tap_col : tap_col + ROW_CELLS]
    return window.reshape(lead + (PLANE_ROWS * ROW_CELLS,))


def stack_at(padded, tap_row, tap_col):
    planes = padded.shape[0] - 2
    moved = plane_shift(padded, tap_row, tap_col)
    return jnp.concatenate(
        [moved[tap_depth : tap_depth + planes] for tap_depth in range(3)], axis=1
    )


def tap_weights(taps, tap_row, tap_col):
    return jnp.concatenate(
        [taps[tap_depth * 9 + tap_row * 3 + tap_col] for tap_depth in range(3)], axis=0
    )


def convolve(padded, taps):
    total = None
    for tap_row in range(3):
        for tap_col in range(3):
            term = jnp.einsum(
                "dcp,co->dop",
                stack_at(padded, tap_row, tap_col),
                tap_weights(taps, tap_row, tap_col),
                preferred_element_type=jnp.float32,
            )
            total = term if total is None else total + term
    return total


def weight_terms(padded, cot_whole, channels):
    pieces = [None] * 27
    for tap_row in range(3):
        for tap_col in range(3):
            block = jnp.einsum(
                "dcp,dop->co",
                stack_at(padded, tap_row, tap_col),
                cot_whole,
                preferred_element_type=jnp.float32,
            )
            block = block.reshape(3, channels, cot_whole.shape[1])
            for tap_depth in range(3):
                pieces[tap_depth * 9 + tap_row * 3 + tap_col] = block[tap_depth]
    return jnp.stack(pieces, axis=0)


def conv_forward(padded, taps):
    planes, channels, cells = padded.shape
    lhs = padded.reshape(1, planes, channels, PLANE_ROWS, ROW_CELLS)
    rhs = taps.reshape(3, 3, 3, channels, taps.shape[-1])
    out = lax.conv_general_dilated(
        lhs, rhs, (1, 1, 1), [(0, 0), (1, 1), (1, 1)],
        dimension_numbers=("NDCHW", "DHWIO", "NDCHW"),
        preferred_element_type=jnp.float32,
    )
    return out.reshape(planes - 2, taps.shape[-1], cells)


def conv_backward(cot_plane, taps):
    planes, channels, cells = cot_plane.shape
    lhs = cot_plane.reshape(1, planes, channels, PLANE_ROWS, ROW_CELLS)
    rhs = taps.reshape(3, 3, 3, taps.shape[1], channels)[::-1, ::-1, ::-1]
    out = lax.conv_general_dilated(
        lhs, rhs, (1, 1, 1), [(2, 2), (1, 1), (1, 1)],
        dimension_numbers=("NDCHW", "DHWOI", "NDCHW"),
        preferred_element_type=jnp.float32,
    )
    return out.reshape(planes + 2, taps.shape[1], cells)


def spill_sum(parts, axis):
    count = lax.axis_size(axis)
    forward = [(i, i + 1) for i in range(count - 1)]
    backward = [(target, source) for source, target in forward]
    from_low = lax.ppermute(parts[-1:], axis, forward)
    from_high = lax.ppermute(parts[:1], axis, backward)
    return parts[1:-1] + from_low + from_high


FLAT_EDGE = 128


def filter_kernel(x_ref, c_ref, o_ref):
    cells = c_ref.shape[0]
    width = x_ref.shape[-1]
    column = lax.broadcasted_iota(jnp.int32, (x_ref.shape[1], cells), 1) % ROW_CELLS
    cot = c_ref[...]
    for tap_depth in range(3):
        plane = x_ref[tap_depth].astype(jnp.float32)
        for tap_row in range(3):
            for tap_col in range(3):
                offset = FLAT_EDGE + (tap_row - 1) * ROW_CELLS + (tap_col - 1)
                moved = pltpu.roll(plane, (width - offset) % width, 1)[:, :cells]
                if tap_col == 0:
                    moved = jnp.where(column >= 1, moved, 0.0)
                if tap_col == 2:
                    moved = jnp.where(column < ROW_CELLS - 1, moved, 0.0)
                o_ref[tap_depth * 9 + tap_row * 3 + tap_col] = jnp.dot(
                    moved.astype(jnp.bfloat16), cot, preferred_element_type=jnp.float32
                )


def conv_filter(padded, cot_whole):
    planes, channels, cells = padded.shape
    flat = jnp.pad(padded, ((0, 0), (0, 0), (FLAT_EDGE, FLAT_EDGE)))
    cot_t = cot_whole[0].T
    return pl.pallas_call(
        filter_kernel,
        out_shape=jax.ShapeDtypeStruct((27, channels, cot_t.shape[1]), jnp.float32),
    )(flat, cot_t)


def scatter_sum(block, axis, dim):
    count = lax.axis_size(axis)
    shape = block.shape
    parts = block.reshape(shape[:dim] + (count, shape[dim] // count) + shape[dim + 1 :])
    parts = jnp.moveaxis(parts, dim, 0)
    parts = lax.all_to_all(parts, axis, 0, 0, tiled=True)
    return parts.sum(axis=0)


def spread_gather(block, axis, dim):
    count = lax.axis_size(axis)
    copies = jnp.broadcast_to(block[None], (count,) + block.shape)
    copies = lax.all_to_all(copies, axis, 0, 0, tiled=True)
    copies = jnp.moveaxis(copies, 0, dim)
    shape = block.shape
    return copies.reshape(shape[:dim] + (count * shape[dim],) + shape[dim + 1 :])


SPACE = ("ylo", "z", "core")


def local(inputs, weights, cotangent):
    padded = extended(inputs, ((SPACE, 0),), 1)
    partial_out = conv_forward(padded, weights)
    chan_masks = partner_masks(lax.axis_size("chan"), 1)[::-1]
    output = halving_sum(partial_out, "chan", chan_masks, 1).astype(jnp.bfloat16)
    gathered = spread_gather(cotangent, "chan", 1)
    input_grad = spill_sum(conv_backward(gathered, weights), SPACE).astype(jnp.bfloat16)
    local_terms = conv_filter(padded, gathered)
    flat = local_terms.reshape(-1, local_terms.shape[-1])
    flat = halving_sum(halving_sum(flat, "core", [1], 0), "ylo", [1], 0)
    flat = spread_gather(scatter_sum(flat, "z", 0), "z", 0)
    flat = doubling_gather(doubling_gather(flat, "ylo", [1], 0), "core", [1], 0)
    weight_grad = flat.reshape(local_terms.shape)
    return (output, input_grad, weight_grad)


def solution(mesh):
    space, chan = mesh.devices.shape
    split = jax.sharding.Mesh(mesh.devices.reshape(2, space // 4, 2, chan), SPACE + ("chan",))
    placed = (P(SPACE, "chan", None), P(None, "chan", None), P(SPACE, "chan", None))
    return jax.shard_map(
        local,
        mesh=split,
        in_specs=placed,
        out_specs=(P(SPACE, "chan", None), P(SPACE, "chan", None), P(None, "chan", None)),
        check_vma=False,
    )
```

```python
import jax
import jax.numpy as jnp
from jax import lax
from jax.sharding import PartitionSpec as P
from jax.experimental import pallas as pl
from jax.experimental.pallas import tpu as pltpu

PLANE_ROWS = 32
ROW_CELLS = 64


def extended(block, sides, width):
    for axis, dim in sides:
        count = lax.axis_size(axis)
        forward = [(i, i + 1) for i in range(count - 1)]
        backward = [(target, source) for source, target in forward]
        low = lax.ppermute(
            lax.slice_in_dim(block, block.shape[dim] - width, None, axis=dim), axis, forward
        )
        high = lax.ppermute(lax.slice_in_dim(block, 0, width, axis=dim), axis, backward)
        block = jnp.concatenate([low, block, high], axis=dim)
    return block


def partner_masks(count, first):
    masks = [1 << b for b in range(count.bit_length() - 1)]
    return [first] + [m for m in masks if m != first]


def halving_sum(block, axis, masks, dim):
    count = lax.axis_size(axis)
    index = lax.axis_index(axis)
    for mask in masks:
        half = block.shape[dim] // 2
        upper = (index // mask) % 2 == 1
        low = lax.slice_in_dim(block, 0, half, axis=dim)
        high = lax.slice_in_dim(block, half, 2 * half, axis=dim)
        keep = jnp.where(upper, high, low)
        send = jnp.where(upper, low, high)
        block = keep + lax.ppermute(send, axis, [(i, i ^ mask) for i in range(count)])
    return block


def doubling_gather(block, axis, masks, dim):
    count = lax.axis_size(axis)
    index = lax.axis_index(axis)
    for mask in masks:
        upper = (index // mask) % 2 == 1
        other = lax.ppermute(block, axis, [(i, i ^ mask) for i in range(count)])
        block = jnp.concatenate(
            [jnp.where(upper, other, block), jnp.where(upper, block, other)], axis=dim
        )
    return block


def plane_shift(field, tap_row, tap_col):
    lead = field.shape[:-1]
    grid = field.reshape(lead + (PLANE_ROWS, ROW_CELLS))
    padded = jnp.pad(grid, [(0, 0)] * len(lead) + [(1, 1), (1, 1)])
    window = padded[..., tap_row : tap_row + PLANE_ROWS, tap_col : tap_col + ROW_CELLS]
    return window.reshape(lead + (PLANE_ROWS * ROW_CELLS,))


def stack_at(padded, tap_row, tap_col):
    planes = padded.shape[0] - 2
    moved = plane_shift(padded, tap_row, tap_col)
    return jnp.concatenate(
        [moved[tap_depth : tap_depth + planes] for tap_depth in range(3)], axis=1
    )


def tap_weights(taps, tap_row, tap_col):
    return jnp.concatenate(
        [taps[tap_depth * 9 + tap_row * 3 + tap_col] for tap_depth in range(3)], axis=0
    )


def convolve(padded, taps):
    total = None
    for tap_row in range(3):
        for tap_col in range(3):
            term = jnp.einsum(
                "dcp,co->dop",
                stack_at(padded, tap_row, tap_col),
                tap_weights(taps, tap_row, tap_col),
                preferred_element_type=jnp.float32,
            )
            total = term if total is None else total + term
    return total


def weight_terms(padded, cot_whole, channels):
    pieces = [None] * 27
    for tap_row in range(3):
        for tap_col in range(3):
            block = jnp.einsum(
                "dcp,dop->co",
                stack_at(padded, tap_row, tap_col),
                cot_whole,
                preferred_element_type=jnp.float32,
            )
            block = block.reshape(3, channels, cot_whole.shape[1])
            for tap_depth in range(3):
                pieces[tap_depth * 9 + tap_row * 3 + tap_col] = block[tap_depth]
    return jnp.stack(pieces, axis=0)


def conv_backward(cot_plane, taps):
    planes, channels, cells = cot_plane.shape
    lhs = cot_plane.reshape(1, planes, channels, PLANE_ROWS, ROW_CELLS)
    rhs = taps.reshape(3, 3, 3, taps.shape[1], channels)[::-1, ::-1, ::-1]
    out = lax.conv_general_dilated(
        lhs, rhs, (1, 1, 1), [(2, 2), (1, 1), (1, 1)],
        dimension_numbers=("NDCHW", "DHWOI", "NDCHW"),
        preferred_element_type=jnp.float32,
    )
    return out.reshape(planes + 2, taps.shape[1], cells)


def spill_sum(parts, axis):
    count = lax.axis_size(axis)
    forward = [(i, i + 1) for i in range(count - 1)]
    backward = [(target, source) for source, target in forward]
    from_low = lax.ppermute(parts[-1:], axis, forward)
    from_high = lax.ppermute(parts[:1], axis, backward)
    return parts[1:-1] + from_low + from_high


FLAT_EDGE = 128


def filter_kernel(x_ref, c_ref, o_ref):
    cells = c_ref.shape[0]
    width = x_ref.shape[-1]
    column = lax.broadcasted_iota(jnp.int32, (x_ref.shape[1], cells), 1) % ROW_CELLS
    cot = c_ref[...]
    for tap_depth in range(3):
        plane = x_ref[tap_depth].astype(jnp.float32)
        for tap_row in range(3):
            for tap_col in range(3):
                offset = FLAT_EDGE + (tap_row - 1) * ROW_CELLS + (tap_col - 1)
                moved = pltpu.roll(plane, (width - offset) % width, 1)[:, :cells]
                if tap_col == 0:
                    moved = jnp.where(column >= 1, moved, 0.0)
                if tap_col == 2:
                    moved = jnp.where(column < ROW_CELLS - 1, moved, 0.0)
                o_ref[tap_depth * 9 + tap_row * 3 + tap_col] = jnp.dot(
                    moved.astype(jnp.bfloat16), cot, preferred_element_type=jnp.float32
                )


def forward_kernel(x_ref, w_ref, o_ref, col_ref):
    cells = o_ref.shape[1]
    width = x_ref.shape[-1]
    channels = x_ref.shape[1]
    column = lax.broadcasted_iota(jnp.int32, (channels, cells), 1) % ROW_CELLS
    for tap_depth in range(3):
        plane = x_ref[tap_depth].astype(jnp.float32)
        for tap_row in range(3):
            for tap_col in range(3):
                offset = FLAT_EDGE + (tap_row - 1) * ROW_CELLS + (tap_col - 1)
                moved = pltpu.roll(plane, (width - offset) % width, 1)[:, :cells]
                if tap_col == 0:
                    moved = jnp.where(column >= 1, moved, 0.0)
                if tap_col == 2:
                    moved = jnp.where(column < ROW_CELLS - 1, moved, 0.0)
                tap = tap_depth * 9 + tap_row * 3 + tap_col
                col_ref[pl.ds(tap * channels, channels), :] = moved.astype(jnp.bfloat16)
    spare = col_ref.shape[0] - 27 * channels
    col_ref[pl.ds(27 * channels, spare), :] = jnp.zeros((spare, cells), jnp.bfloat16)
    o_ref[...] = jnp.dot(w_ref[...], col_ref[...], preferred_element_type=jnp.float32)


def conv_forward(padded, taps):
    planes, channels, cells = padded.shape
    flat = jnp.pad(padded, ((0, 0), (0, 0), (FLAT_EDGE, FLAT_EDGE)))
    rows = 27 * channels
    depth = -(-rows // 128) * 128
    lhs = jnp.pad(taps.reshape(rows, taps.shape[-1]), ((0, depth - rows), (0, 0))).T
    out = pl.pallas_call(
        forward_kernel,
        out_shape=jax.ShapeDtypeStruct((taps.shape[-1], cells), jnp.float32),
        scratch_shapes=[pltpu.VMEM((depth, cells), jnp.bfloat16)],
    )(flat, lhs)
    return out.reshape(planes - 2, taps.shape[-1], cells)


def conv_filter(padded, cot_whole):
    planes, channels, cells = padded.shape
    flat = jnp.pad(padded, ((0, 0), (0, 0), (FLAT_EDGE, FLAT_EDGE)))
    cot_t = cot_whole[0].T
    return pl.pallas_call(
        filter_kernel,
        out_shape=jax.ShapeDtypeStruct((27, channels, cot_t.shape[1]), jnp.float32),
    )(flat, cot_t)


def scatter_sum(block, axis, dim):
    count = lax.axis_size(axis)
    shape = block.shape
    parts = block.reshape(shape[:dim] + (count, shape[dim] // count) + shape[dim + 1 :])
    parts = jnp.moveaxis(parts, dim, 0)
    parts = lax.all_to_all(parts, axis, 0, 0, tiled=True)
    return parts.sum(axis=0)


def spread_gather(block, axis, dim):
    count = lax.axis_size(axis)
    copies = jnp.broadcast_to(block[None], (count,) + block.shape)
    copies = lax.all_to_all(copies, axis, 0, 0, tiled=True)
    copies = jnp.moveaxis(copies, 0, dim)
    shape = block.shape
    return copies.reshape(shape[:dim] + (count * shape[dim],) + shape[dim + 1 :])


SPACE = ("srest", "core")


def local(inputs, weights, cotangent):
    padded = extended(inputs, ((SPACE, 0),), 1)
    partial_out = conv_forward(padded, weights)
    chan_masks = partner_masks(lax.axis_size("chan"), 1)[::-1]
    output = halving_sum(partial_out, "chan", chan_masks, 1).astype(jnp.bfloat16)
    gathered = spread_gather(cotangent, "chan", 1)
    input_grad = spill_sum(conv_backward(gathered, weights), SPACE).astype(jnp.bfloat16)
    local_terms = conv_filter(padded, gathered)
    flat = local_terms.reshape(-1, local_terms.shape[-1])
    flat = halving_sum(flat, "core", [1], 0)
    flat = spread_gather(scatter_sum(flat, "srest", 0), "srest", 0)
    flat = doubling_gather(flat, "core", [1], 0)
    weight_grad = flat.reshape(local_terms.shape)
    return (output, input_grad, weight_grad)


def solution(mesh):
    space, chan = mesh.devices.shape
    split = jax.sharding.Mesh(mesh.devices.reshape(space // 2, 2, chan), SPACE + ("chan",))
    placed = (P(SPACE, "chan", None), P(None, "chan", None), P(SPACE, "chan", None))
    return jax.shard_map(
        local,
        mesh=split,
        in_specs=placed,
        out_specs=(P(SPACE, "chan", None), P(SPACE, "chan", None), P(None, "chan", None)),
        check_vma=False,
    )
```

```python
import jax
import jax.numpy as jnp
from jax import lax
from jax.sharding import PartitionSpec as P
from jax.experimental import pallas as pl
from jax.experimental.pallas import tpu as pltpu

PLANE_ROWS = 32
ROW_CELLS = 64


def extended(block, sides, width):
    for axis, dim in sides:
        count = lax.axis_size(axis)
        forward = [(i, i + 1) for i in range(count - 1)]
        backward = [(target, source) for source, target in forward]
        low = lax.ppermute(
            lax.slice_in_dim(block, block.shape[dim] - width, None, axis=dim), axis, forward
        )
        high = lax.ppermute(lax.slice_in_dim(block, 0, width, axis=dim), axis, backward)
        block = jnp.concatenate([low, block, high], axis=dim)
    return block


def partner_masks(count, first):
    masks = [1 << b for b in range(count.bit_length() - 1)]
    return [first] + [m for m in masks if m != first]


def halving_sum(block, axis, masks, dim):
    count = lax.axis_size(axis)
    index = lax.axis_index(axis)
    for mask in masks:
        half = block.shape[dim] // 2
        upper = (index // mask) % 2
        keep = lax.dynamic_slice_in_dim(block, upper * half, half, axis=dim)
        send = lax.dynamic_slice_in_dim(block, (1 - upper) * half, half, axis=dim)
        block = keep + lax.ppermute(send, axis, [(i, i ^ mask) for i in range(count)])
    return block


def doubling_gather(block, axis, masks, dim):
    count = lax.axis_size(axis)
    index = lax.axis_index(axis)
    for mask in masks:
        upper = (index // mask) % 2 == 1
        other = lax.ppermute(block, axis, [(i, i ^ mask) for i in range(count)])
        block = jnp.concatenate(
            [jnp.where(upper, other, block), jnp.where(upper, block, other)], axis=dim
        )
    return block


def plane_shift(field, tap_row, tap_col):
    lead = field.shape[:-1]
    grid = field.reshape(lead + (PLANE_ROWS, ROW_CELLS))
    padded = jnp.pad(grid, [(0, 0)] * len(lead) + [(1, 1), (1, 1)])
    window = padded[..., tap_row : tap_row + PLANE_ROWS, tap_col : tap_col + ROW_CELLS]
    return window.reshape(lead + (PLANE_ROWS * ROW_CELLS,))


def stack_at(padded, tap_row, tap_col):
    planes = padded.shape[0] - 2
    moved = plane_shift(padded, tap_row, tap_col)
    return jnp.concatenate(
        [moved[tap_depth : tap_depth + planes] for tap_depth in range(3)], axis=1
    )


def tap_weights(taps, tap_row, tap_col):
    return jnp.concatenate(
        [taps[tap_depth * 9 + tap_row * 3 + tap_col] for tap_depth in range(3)], axis=0
    )


def convolve(padded, taps):
    total = None
    for tap_row in range(3):
        for tap_col in range(3):
            term = jnp.einsum(
                "dcp,co->dop",
                stack_at(padded, tap_row, tap_col),
                tap_weights(taps, tap_row, tap_col),
                preferred_element_type=jnp.float32,
            )
            total = term if total is None else total + term
    return total


def weight_terms(padded, cot_whole, channels):
    pieces = [None] * 27
    for tap_row in range(3):
        for tap_col in range(3):
            block = jnp.einsum(
                "dcp,dop->co",
                stack_at(padded, tap_row, tap_col),
                cot_whole,
                preferred_element_type=jnp.float32,
            )
            block = block.reshape(3, channels, cot_whole.shape[1])
            for tap_depth in range(3):
                pieces[tap_depth * 9 + tap_row * 3 + tap_col] = block[tap_depth]
    return jnp.stack(pieces, axis=0)


def conv_forward(padded, taps):
    planes, channels, cells = padded.shape
    lhs = padded.reshape(1, planes, channels, PLANE_ROWS, ROW_CELLS)
    rhs = taps.reshape(3, 3, 3, channels, taps.shape[-1])
    out = lax.conv_general_dilated(
        lhs, rhs, (1, 1, 1), [(0, 0), (1, 1), (1, 1)],
        dimension_numbers=("NDCHW", "DHWIO", "NDCHW"),
        preferred_element_type=jnp.float32,
    )
    return out.reshape(planes - 2, taps.shape[-1], cells)


def conv_backward(cot_plane, taps):
    planes, channels, cells = cot_plane.shape
    lhs = cot_plane.reshape(1, planes, channels, PLANE_ROWS, ROW_CELLS)
    rhs = taps.reshape(3, 3, 3, taps.shape[1], channels)[::-1, ::-1, ::-1]
    out = lax.conv_general_dilated(
        lhs, rhs, (1, 1, 1), [(2, 2), (1, 1), (1, 1)],
        dimension_numbers=("NDCHW", "DHWOI", "NDCHW"),
        preferred_element_type=jnp.float32,
    )
    return out.reshape(planes + 2, taps.shape[1], cells)


def spill_sum(parts, axis):
    count = lax.axis_size(axis)
    forward = [(i, i + 1) for i in range(count - 1)]
    backward = [(target, source) for source, target in forward]
    from_low = lax.ppermute(parts[-1:], axis, forward)
    from_high = lax.ppermute(parts[:1], axis, backward)
    return parts[1:-1] + from_low + from_high


FLAT_EDGE = 128


def filter_kernel(x_ref, c_ref, o_ref):
    cells = c_ref.shape[0]
    width = x_ref.shape[-1]
    column = lax.broadcasted_iota(jnp.int32, (x_ref.shape[1], cells), 1) % ROW_CELLS
    cot = c_ref[...]
    for tap_depth in range(3):
        plane = x_ref[tap_depth].astype(jnp.float32)
        for tap_row in range(3):
            for tap_col in range(3):
                offset = FLAT_EDGE + (tap_row - 1) * ROW_CELLS + (tap_col - 1)
                moved = pltpu.roll(plane, (width - offset) % width, 1)[:, :cells]
                if tap_col == 0:
                    moved = jnp.where(column >= 1, moved, 0.0)
                if tap_col == 2:
                    moved = jnp.where(column < ROW_CELLS - 1, moved, 0.0)
                o_ref[tap_depth * 9 + tap_row * 3 + tap_col] = jnp.dot(
                    moved.astype(jnp.bfloat16), cot, preferred_element_type=jnp.float32
                )


def conv_filter(padded, cot_whole):
    planes, channels, cells = padded.shape
    flat = jnp.pad(padded, ((0, 0), (0, 0), (FLAT_EDGE, FLAT_EDGE)))
    cot_t = cot_whole[0].T
    return pl.pallas_call(
        filter_kernel,
        out_shape=jax.ShapeDtypeStruct((27, channels, cot_t.shape[1]), jnp.float32),
    )(flat, cot_t)


def scatter_sum(block, axis, dim):
    count = lax.axis_size(axis)
    shape = block.shape
    parts = block.reshape(shape[:dim] + (count, shape[dim] // count) + shape[dim + 1 :])
    parts = jnp.moveaxis(parts, dim, 0)
    parts = lax.all_to_all(parts, axis, 0, 0, tiled=True)
    return parts.sum(axis=0)


def spread_gather(block, axis, dim):
    count = lax.axis_size(axis)
    copies = jnp.broadcast_to(block[None], (count,) + block.shape)
    copies = lax.all_to_all(copies, axis, 0, 0, tiled=True)
    copies = jnp.moveaxis(copies, 0, dim)
    shape = block.shape
    return copies.reshape(shape[:dim] + (count * shape[dim],) + shape[dim + 1 :])


SPACE = ("srest", "core")


def local(inputs, weights, cotangent):
    padded = extended(inputs, ((SPACE, 0),), 1)
    partial_out = conv_forward(padded, weights)
    chan_masks = partner_masks(lax.axis_size("chan"), 1)[::-1]
    output = halving_sum(partial_out, "chan", chan_masks, 1).astype(jnp.bfloat16)
    gathered = spread_gather(cotangent, "chan", 1)
    input_grad = spill_sum(conv_backward(gathered, weights), SPACE).astype(jnp.bfloat16)
    local_terms = conv_filter(padded, gathered)
    flat = local_terms.reshape(-1, local_terms.shape[-1])
    flat = halving_sum(flat, "core", [1], 0)
    flat = spread_gather(scatter_sum(flat, "srest", 0), "srest", 0)
    flat = doubling_gather(flat, "core", [1], 0)
    weight_grad = flat.reshape(local_terms.shape)
    return (output, input_grad, weight_grad)


def solution(mesh):
    space, chan = mesh.devices.shape
    split = jax.sharding.Mesh(mesh.devices.reshape(space // 2, 2, chan), SPACE + ("chan",))
    placed = (P(SPACE, "chan", None), P(None, "chan", None), P(SPACE, "chan", None))
    return jax.shard_map(
        local,
        mesh=split,
        in_specs=placed,
        out_specs=(P(SPACE, "chan", None), P(SPACE, "chan", None), P(None, "chan", None)),
        check_vma=False,
    )
```

```python
import jax
import jax.numpy as jnp
from jax import lax
from jax.sharding import PartitionSpec as P
from jax.experimental import pallas as pl
from jax.experimental.pallas import tpu as pltpu

PLANE_ROWS = 32
ROW_CELLS = 64


def extended(block, sides, width):
    for axis, dim in sides:
        count = lax.axis_size(axis)
        forward = [(i, i + 1) for i in range(count - 1)]
        backward = [(target, source) for source, target in forward]
        low = lax.ppermute(
            lax.slice_in_dim(block, block.shape[dim] - width, None, axis=dim), axis, forward
        )
        high = lax.ppermute(lax.slice_in_dim(block, 0, width, axis=dim), axis, backward)
        block = jnp.concatenate([low, block, high], axis=dim)
    return block


def partner_masks(count, first):
    masks = [1 << b for b in range(count.bit_length() - 1)]
    return [first] + [m for m in masks if m != first]


def halving_sum(block, axis, masks, dim):
    count = lax.axis_size(axis)
    index = lax.axis_index(axis)
    for mask in masks:
        half = block.shape[dim] // 2
        upper = (index // mask) % 2 == 1
        low = lax.slice_in_dim(block, 0, half, axis=dim)
        high = lax.slice_in_dim(block, half, 2 * half, axis=dim)
        keep = jnp.where(upper, high, low)
        send = jnp.where(upper, low, high)
        block = keep + lax.ppermute(send, axis, [(i, i ^ mask) for i in range(count)])
    return block


def doubling_gather(block, axis, masks, dim):
    count = lax.axis_size(axis)
    index = lax.axis_index(axis)
    for mask in masks:
        upper = (index // mask) % 2 == 1
        other = lax.ppermute(block, axis, [(i, i ^ mask) for i in range(count)])
        block = jnp.concatenate(
            [jnp.where(upper, other, block), jnp.where(upper, block, other)], axis=dim
        )
    return block


def plane_shift(field, tap_row, tap_col):
    lead = field.shape[:-1]
    grid = field.reshape(lead + (PLANE_ROWS, ROW_CELLS))
    padded = jnp.pad(grid, [(0, 0)] * len(lead) + [(1, 1), (1, 1)])
    window = padded[..., tap_row : tap_row + PLANE_ROWS, tap_col : tap_col + ROW_CELLS]
    return window.reshape(lead + (PLANE_ROWS * ROW_CELLS,))


def stack_at(padded, tap_row, tap_col):
    planes = padded.shape[0] - 2
    moved = plane_shift(padded, tap_row, tap_col)
    return jnp.concatenate(
        [moved[tap_depth : tap_depth + planes] for tap_depth in range(3)], axis=1
    )


def tap_weights(taps, tap_row, tap_col):
    return jnp.concatenate(
        [taps[tap_depth * 9 + tap_row * 3 + tap_col] for tap_depth in range(3)], axis=0
    )


def convolve(padded, taps):
    total = None
    for tap_row in range(3):
        for tap_col in range(3):
            term = jnp.einsum(
                "dcp,co->dop",
                stack_at(padded, tap_row, tap_col),
                tap_weights(taps, tap_row, tap_col),
                preferred_element_type=jnp.float32,
            )
            total = term if total is None else total + term
    return total


def weight_terms(padded, cot_whole, channels):
    pieces = [None] * 27
    for tap_row in range(3):
        for tap_col in range(3):
            block = jnp.einsum(
                "dcp,dop->co",
                stack_at(padded, tap_row, tap_col),
                cot_whole,
                preferred_element_type=jnp.float32,
            )
            block = block.reshape(3, channels, cot_whole.shape[1])
            for tap_depth in range(3):
                pieces[tap_depth * 9 + tap_row * 3 + tap_col] = block[tap_depth]
    return jnp.stack(pieces, axis=0)


def conv_forward(padded, taps):
    planes, channels, cells = padded.shape
    lhs = padded.reshape(1, planes, channels, PLANE_ROWS, ROW_CELLS)
    rhs = taps.reshape(3, 3, 3, channels, taps.shape[-1])
    out = lax.conv_general_dilated(
        lhs, rhs, (1, 1, 1), [(0, 0), (1, 1), (1, 1)],
        dimension_numbers=("NDCHW", "DHWIO", "NDCHW"),
        preferred_element_type=jnp.float32,
    )
    return out.reshape(planes - 2, taps.shape[-1], cells)


def conv_backward(cot_plane, taps):
    planes, channels, cells = cot_plane.shape
    lhs = cot_plane.reshape(1, planes, channels, PLANE_ROWS, ROW_CELLS)
    rhs = taps.reshape(3, 3, 3, taps.shape[1], channels)[::-1, ::-1, ::-1]
    out = lax.conv_general_dilated(
        lhs, rhs, (1, 1, 1), [(2, 2), (1, 1), (1, 1)],
        dimension_numbers=("NDCHW", "DHWOI", "NDCHW"),
        preferred_element_type=jnp.float32,
    )
    return out.reshape(planes + 2, taps.shape[1], cells)


def spill_sum(parts, axis):
    count = lax.axis_size(axis)
    forward = [(i, i + 1) for i in range(count - 1)]
    backward = [(target, source) for source, target in forward]
    from_low = lax.ppermute(parts[-1:], axis, forward)
    from_high = lax.ppermute(parts[:1], axis, backward)
    return parts[1:-1] + from_low + from_high


FLAT_EDGE = 128


def filter_kernel(x_ref, c_ref, o_ref):
    cells = c_ref.shape[0]
    width = x_ref.shape[-1]
    column = lax.broadcasted_iota(jnp.int32, (x_ref.shape[1], cells), 1) % ROW_CELLS
    cot = c_ref[...]
    for tap_depth in range(3):
        plane = x_ref[tap_depth].astype(jnp.float32)
        for tap_row in range(3):
            for tap_col in range(3):
                offset = FLAT_EDGE + (tap_row - 1) * ROW_CELLS + (tap_col - 1)
                moved = pltpu.roll(plane, (width - offset) % width, 1)[:, :cells]
                if tap_col == 0:
                    moved = jnp.where(column >= 1, moved, 0.0)
                if tap_col == 2:
                    moved = jnp.where(column < ROW_CELLS - 1, moved, 0.0)
                o_ref[tap_depth * 9 + tap_row * 3 + tap_col] = jnp.dot(
                    moved.astype(jnp.bfloat16), cot, preferred_element_type=jnp.float32
                )


def conv_filter(padded, cot_whole):
    planes, channels, cells = padded.shape
    flat = jnp.pad(padded, ((0, 0), (0, 0), (FLAT_EDGE, FLAT_EDGE)))
    cot_t = cot_whole[0].T
    return pl.pallas_call(
        filter_kernel,
        out_shape=jax.ShapeDtypeStruct((27, channels, cot_t.shape[1]), jnp.float32),
    )(flat, cot_t)


def scatter_sum(block, axis, dim):
    count = lax.axis_size(axis)
    shape = block.shape
    parts = block.reshape(shape[:dim] + (count, shape[dim] // count) + shape[dim + 1 :])
    parts = jnp.moveaxis(parts, dim, 0)
    parts = lax.all_to_all(parts, axis, 0, 0, tiled=True)
    return parts.sum(axis=0)


def spread_gather(block, axis, dim):
    count = lax.axis_size(axis)
    copies = jnp.broadcast_to(block[None], (count,) + block.shape)
    copies = lax.all_to_all(copies, axis, 0, 0, tiled=True)
    copies = jnp.moveaxis(copies, 0, dim)
    shape = block.shape
    return copies.reshape(shape[:dim] + (count * shape[dim],) + shape[dim + 1 :])


SPACE = ("srest", "core")


def local(inputs, weights, cotangent):
    padded = extended(inputs, ((SPACE, 0),), 1)
    chan_count = lax.axis_size("chan")
    chan_masks = partner_masks(chan_count, min(2, chan_count // 2))
    chan_masks = [chan_masks[0]] + sorted(chan_masks[1:], reverse=True)
    order = [0] * chan_count
    for index in range(chan_count):
        place = 0
        for mask in chan_masks:
            place = place * 2 + (index // mask) % 2
        order[place] = index
    kinds, rows, cols = weights.shape
    ordered = weights.reshape(kinds, rows, chan_count, cols // chan_count)[:, :, jnp.array(order), :]
    partial_out = conv_forward(padded, ordered.reshape(kinds, rows, cols))
    output = halving_sum(partial_out, "chan", chan_masks, 1).astype(jnp.bfloat16)
    gathered = spread_gather(cotangent, "chan", 1)
    input_grad = spill_sum(conv_backward(gathered, weights), SPACE).astype(jnp.bfloat16)
    local_terms = conv_filter(padded, gathered)
    flat = local_terms.reshape(-1, local_terms.shape[-1])
    flat = halving_sum(flat, "core", [1], 0)
    flat = spread_gather(scatter_sum(flat, "srest", 0), "srest", 0)
    flat = doubling_gather(flat, "core", [1], 0)
    weight_grad = flat.reshape(local_terms.shape)
    return (output, input_grad, weight_grad)


def solution(mesh):
    space, chan = mesh.devices.shape
    split = jax.sharding.Mesh(mesh.devices.reshape(space // 2, 2, chan), SPACE + ("chan",))
    placed = (P(SPACE, "chan", None), P(None, "chan", None), P(SPACE, "chan", None))
    return jax.shard_map(
        local,
        mesh=split,
        in_specs=placed,
        out_specs=(P(SPACE, "chan", None), P(SPACE, "chan", None), P(None, "chan", None)),
        check_vma=False,
    )
```

```python
import jax
import jax.numpy as jnp
from jax import lax
from jax.sharding import PartitionSpec as P
from jax.experimental import pallas as pl
from jax.experimental.pallas import tpu as pltpu

PLANE_ROWS = 32
ROW_CELLS = 64


def extended(block, sides, width):
    for axis, dim in sides:
        count = lax.axis_size(axis)
        forward = [(i, i + 1) for i in range(count - 1)]
        backward = [(target, source) for source, target in forward]
        low = lax.ppermute(
            lax.slice_in_dim(block, block.shape[dim] - width, None, axis=dim), axis, forward
        )
        high = lax.ppermute(lax.slice_in_dim(block, 0, width, axis=dim), axis, backward)
        block = jnp.concatenate([low, block, high], axis=dim)
    return block


def partner_masks(count, first):
    masks = [1 << b for b in range(count.bit_length() - 1)]
    return [first] + [m for m in masks if m != first]


def halving_sum(block, axis, masks, dim):
    count = lax.axis_size(axis)
    index = lax.axis_index(axis)
    for mask in masks:
        half = block.shape[dim] // 2
        upper = (index // mask) % 2 == 1
        low = lax.slice_in_dim(block, 0, half, axis=dim)
        high = lax.slice_in_dim(block, half, 2 * half, axis=dim)
        keep = jnp.where(upper, high, low)
        send = jnp.where(upper, low, high)
        block = keep + lax.ppermute(send, axis, [(i, i ^ mask) for i in range(count)])
    return block


def doubling_gather(block, axis, masks, dim):
    count = lax.axis_size(axis)
    index = lax.axis_index(axis)
    for mask in masks:
        upper = (index // mask) % 2 == 1
        other = lax.ppermute(block, axis, [(i, i ^ mask) for i in range(count)])
        block = jnp.concatenate(
            [jnp.where(upper, other, block), jnp.where(upper, block, other)], axis=dim
        )
    return block


def plane_shift(field, tap_row, tap_col):
    lead = field.shape[:-1]
    grid = field.reshape(lead + (PLANE_ROWS, ROW_CELLS))
    padded = jnp.pad(grid, [(0, 0)] * len(lead) + [(1, 1), (1, 1)])
    window = padded[..., tap_row : tap_row + PLANE_ROWS, tap_col : tap_col + ROW_CELLS]
    return window.reshape(lead + (PLANE_ROWS * ROW_CELLS,))


def stack_at(padded, tap_row, tap_col):
    planes = padded.shape[0] - 2
    moved = plane_shift(padded, tap_row, tap_col)
    return jnp.concatenate(
        [moved[tap_depth : tap_depth + planes] for tap_depth in range(3)], axis=1
    )


def tap_weights(taps, tap_row, tap_col):
    return jnp.concatenate(
        [taps[tap_depth * 9 + tap_row * 3 + tap_col] for tap_depth in range(3)], axis=0
    )


def convolve(padded, taps):
    total = None
    for tap_row in range(3):
        for tap_col in range(3):
            term = jnp.einsum(
                "dcp,co->dop",
                stack_at(padded, tap_row, tap_col),
                tap_weights(taps, tap_row, tap_col),
                preferred_element_type=jnp.float32,
            )
            total = term if total is None else total + term
    return total


def weight_terms(padded, cot_whole, channels):
    pieces = [None] * 27
    for tap_row in range(3):
        for tap_col in range(3):
            block = jnp.einsum(
                "dcp,dop->co",
                stack_at(padded, tap_row, tap_col),
                cot_whole,
                preferred_element_type=jnp.float32,
            )
            block = block.reshape(3, channels, cot_whole.shape[1])
            for tap_depth in range(3):
                pieces[tap_depth * 9 + tap_row * 3 + tap_col] = block[tap_depth]
    return jnp.stack(pieces, axis=0)


def conv_forward(padded, taps):
    planes, channels, cells = padded.shape
    lhs = padded.reshape(1, planes, channels, PLANE_ROWS, ROW_CELLS)
    rhs = taps.reshape(3, 3, 3, channels, taps.shape[-1])
    out = lax.conv_general_dilated(
        lhs, rhs, (1, 1, 1), [(0, 0), (1, 1), (1, 1)],
        dimension_numbers=("NDCHW", "DHWIO", "NDCHW"),
        preferred_element_type=jnp.float32,
    )
    return out.reshape(planes - 2, taps.shape[-1], cells)


def conv_backward(cot_plane, taps):
    planes, channels, cells = cot_plane.shape
    lhs = cot_plane.reshape(1, planes, channels, PLANE_ROWS, ROW_CELLS)
    rhs = taps.reshape(3, 3, 3, taps.shape[1], channels)[::-1, ::-1, ::-1]
    out = lax.conv_general_dilated(
        lhs, rhs, (1, 1, 1), [(2, 2), (1, 1), (1, 1)],
        dimension_numbers=("NDCHW", "DHWOI", "NDCHW"),
        preferred_element_type=jnp.float32,
    )
    return out.reshape(planes + 2, taps.shape[1], cells)


def spill_sum(parts, axis):
    count = lax.axis_size(axis)
    forward = [(i, i + 1) for i in range(count - 1)]
    backward = [(target, source) for source, target in forward]
    from_low = lax.ppermute(parts[-1:], axis, forward)
    from_high = lax.ppermute(parts[:1], axis, backward)
    return parts[1:-1] + from_low + from_high


FLAT_EDGE = 128


def filter_kernel(x_ref, c_ref, o_ref):
    cells = c_ref.shape[0]
    width = x_ref.shape[-1]
    column = lax.broadcasted_iota(jnp.int32, (x_ref.shape[1], cells), 1) % ROW_CELLS
    cot = c_ref[...]
    for tap_depth in range(3):
        plane = x_ref[tap_depth].astype(jnp.float32)
        for tap_row in range(3):
            for tap_col in range(3):
                offset = FLAT_EDGE + (tap_row - 1) * ROW_CELLS + (tap_col - 1)
                moved = pltpu.roll(plane, (width - offset) % width, 1)[:, :cells]
                if tap_col == 0:
                    moved = jnp.where(column >= 1, moved, 0.0)
                if tap_col == 2:
                    moved = jnp.where(column < ROW_CELLS - 1, moved, 0.0)
                o_ref[tap_depth * 9 + tap_row * 3 + tap_col] = jnp.dot(
                    moved.astype(jnp.bfloat16), cot, preferred_element_type=jnp.float32
                )


def conv_filter(padded, cot_whole):
    planes, channels, cells = padded.shape
    flat = jnp.pad(padded, ((0, 0), (0, 0), (FLAT_EDGE, FLAT_EDGE)))
    cot_t = cot_whole[0].T
    return pl.pallas_call(
        filter_kernel,
        out_shape=jax.ShapeDtypeStruct((27, channels, cot_t.shape[1]), jnp.float32),
    )(flat, cot_t)


def scatter_sum(block, axis, dim):
    count = lax.axis_size(axis)
    shape = block.shape
    parts = block.reshape(shape[:dim] + (count, shape[dim] // count) + shape[dim + 1 :])
    parts = jnp.moveaxis(parts, dim, 0)
    parts = lax.all_to_all(parts, axis, 0, 0, tiled=True)
    return parts.sum(axis=0)


def spread_gather(block, axis, dim):
    count = lax.axis_size(axis)
    copies = jnp.broadcast_to(block[None], (count,) + block.shape)
    copies = lax.all_to_all(copies, axis, 0, 0, tiled=True)
    copies = jnp.moveaxis(copies, 0, dim)
    shape = block.shape
    return copies.reshape(shape[:dim] + (count * shape[dim],) + shape[dim + 1 :])


SPACE = ("srest", "core")


def local(inputs, weights, cotangent):
    padded = extended(inputs, ((SPACE, 0),), 1)
    chan_count = lax.axis_size("chan")
    chan_masks = partner_masks(chan_count, 1)
    chan_masks = [chan_masks[0]] + sorted(chan_masks[1:], reverse=True)
    order = [0] * chan_count
    for index in range(chan_count):
        place = 0
        for mask in chan_masks:
            place = place * 2 + (index // mask) % 2
        order[place] = index
    kinds, rows, cols = weights.shape
    ordered = weights.reshape(kinds, rows, chan_count, cols // chan_count)[:, :, jnp.array(order), :]
    partial_out = conv_forward(padded, ordered.reshape(kinds, rows, cols))
    output = halving_sum(partial_out, "chan", chan_masks, 1).astype(jnp.bfloat16)
    gathered = spread_gather(cotangent, "chan", 1)
    input_grad = spill_sum(conv_backward(gathered, weights), SPACE).astype(jnp.bfloat16)
    local_terms = conv_filter(padded, gathered)
    flat = local_terms.reshape(-1, local_terms.shape[-1])
    flat = halving_sum(flat, "core", [1], 0)
    flat = spread_gather(scatter_sum(flat, "srest", 0), "srest", 0)
    flat = doubling_gather(flat, "core", [1], 0)
    weight_grad = flat.reshape(local_terms.shape)
    return (output, input_grad, weight_grad)


def solution(mesh):
    space, chan = mesh.devices.shape
    split = jax.sharding.Mesh(mesh.devices.reshape(space // 2, 2, chan), SPACE + ("chan",))
    placed = (P(SPACE, "chan", None), P(None, "chan", None), P(SPACE, "chan", None))
    return jax.shard_map(
        local,
        mesh=split,
        in_specs=placed,
        out_specs=(P(SPACE, "chan", None), P(SPACE, "chan", None), P(None, "chan", None)),
        check_vma=False,
    )
```
